128 devices in a mesh: seq: 64 (over z_hi, y, x, core), mp: 2 (over z_lo).
Axes of the slice: x: 4, y: 4, z: 4 (z_hi: 2, z_lo: 2; z = z_hi * 2 + z_lo), core: 2. Of those that a mesh axis runs over, the one named last changes fastest.
Arguments:
- residual_in: bfloat16 [65536, 1024], P('seq'), may hold values from -6 to 6
- query_rows: bfloat16 [65536, 1024], P('seq', 'mp'), may hold values from -6 to 6
- key_rows: bfloat16 [65536, 1024], P('seq', 'mp'), may hold values from -6 to 6
- value_rows: bfloat16 [65536, 1024], P('seq', 'mp'), may hold values from -6 to 6
- rand_blocks: int32 [1024, 16, 3], P(None, 'mp'), may hold values from 0 to 1023, as said below
- global_blocks: int32 [2], replicated, may hold values from 0 to 1023, as said below
- out_weight: bfloat16 [1024, 1024], P('mp'), may hold values from -0.1875 to 0.1875
- norm_gain: float32 [1024], replicated, may hold values from 0.25 to 1.75
- up_weight: bfloat16 [1024, 4096], P(None, 'mp'), may hold values from -0.1875 to 0.1875
- down_weight: bfloat16 [4096, 1024], P('mp'), may hold values from -0.09375 to 0.09375
Outputs:
- layer_out: bfloat16 [65536, 1024], P('seq', 'mp')
The draws below stay inside these ranges and needn't reach their ends.
Inputs may be any that keep to these rules, and one draw needn't show every extreme that they name: `rand_blocks`: each entry names a block of the same run of 16 consecutive groups of 16 blocks as its query block (groups counted from block 0). For every group of 16 query blocks, every set of 8 consecutive heads starting at a multiple of 8, and every group of its run, exactly 24 entries point into that group. `global_blocks`: the 2 entries differ; the last one is block 1023.
All inputs are finite; a program needn't handle non-finite values.
Results may differ from the reference program's by a relative error of at most 0.006.
Values may be sent and summed in bfloat16 or wider, within the bound.
No kernel may reach another device: no remote copies, remote signals or barrier semaphores. Data moves between devices by JAX's collectives and lax.ppermute only.
A program may use at most 256 MiB of HBM per device.

```python
import math
import jax
import jax.numpy as jnp
from jax import lax

D = 1024
H = 16
HD = 64
FF = 4096
BLK = 64
R = 3
GLOB = 2
GROUP = 16
QB_DEV = 16
TOK_DEV = 1024
NB = 1024
TOKENS = 65536
HEADS_DEV = 8


def run_numbers():
    return jnp.arange(TOKENS, dtype=jnp.int32) // TOK_DEV


def draw_query_rows(key, part):
    drawn_draw = jnp.clip(jax.random.normal(jax.random.fold_in(key, 1), (TOKENS, D), jnp.float32), -4.5, 4.5)
    return drawn_draw.astype(jnp.bfloat16)


def draw_key_rows(key, part):
    drawn_draw = jnp.clip(jax.random.normal(jax.random.fold_in(key, 2), (TOKENS, D), jnp.float32), -4.5, 4.5)
    run_count = NB // QB_DEV
    run_shift = jax.random.uniform(jax.random.fold_in(key, 8), (run_count,), jnp.float32, -2.0, 2.0)
    direction = 2.0 * jax.random.randint(jax.random.fold_in(key, 9), (D,), 0, 2).astype(jnp.float32) - 1.0
    drawn_draw = jnp.clip(drawn_draw + run_shift[run_numbers()][:, None] * direction[None, :], -6.0, 6.0)
    return drawn_draw.astype(jnp.bfloat16)


def draw_value_rows(key, part):
    run_count = NB // QB_DEV
    drawn_draw = jnp.clip(jax.random.normal(jax.random.fold_in(key, 10), (TOKENS, D), jnp.float32), -4.5, 4.5)
    run_offset = jax.random.uniform(jax.random.fold_in(key, 11), (run_count, D), jnp.float32, -1.5, 1.5)
    return jnp.clip(drawn_draw + run_offset[run_numbers()], -6.0, 6.0).astype(jnp.bfloat16)


def draw_rand_blocks(key, part):
    shard_count = NB // QB_DEV
    halves = H // HEADS_DEV
    slot_count = QB_DEV * HEADS_DEV * R
    capacity = slot_count // GROUP
    key_list = jax.random.split(jax.random.fold_in(key, 3), shard_count * halves)
    slot_order = jax.vmap(lambda single_key: jax.random.permutation(single_key, slot_count))(key_list)
    offset_table = slot_order // capacity
    inner_block = jax.random.randint(jax.random.fold_in(key, 4), (shard_count * halves, slot_count), 0, QB_DEV)
    shard_ids = jnp.repeat(jnp.arange(shard_count, dtype=jnp.int32), halves)
    position = shard_ids % GROUP
    owner_shard = (shard_ids - position)[:, None] + (position[:, None] + offset_table) % GROUP
    block_table = owner_shard * QB_DEV + inner_block
    block_table = block_table.reshape(shard_count, halves, QB_DEV, HEADS_DEV, R).transpose(0, 2, 1, 3, 4).reshape(NB, H, R)
    return block_table.astype(jnp.int32)


def draw_global_blocks(key, part):
    first_block = jax.random.randint(jax.random.fold_in(key, 5), (), 0, NB - 1)
    return jnp.stack([first_block, jnp.array(NB - 1, dtype=jnp.int32)]).astype(jnp.int32)


def block_scale(rng, shape, shards, least, largest):
    loudness, own = 1.0, jax.random.fold_in(rng, 6)
    for axis_at, shards_of in shards:
        heights = jnp.exp(jax.random.uniform(jax.random.fold_in(own, axis_at), (shards_of,), jnp.float32, least / len(shards), largest / len(shards)))
        loudness = loudness * jnp.repeat(heights, shape[axis_at] // shards_of).reshape([-1 if axis == axis_at else 1 for axis in range(len(shape))])
    return loudness


def scatter_about(own_key, dims, width, reach, shards=(), kind=jnp.bfloat16):
    values = width * jax.random.normal(own_key, dims, jnp.float32)
    if shards:
        values = values * block_scale(own_key, dims, shards, -0.22, 0.18)
    return jnp.clip(values, -reach, reach).astype(kind)


def setup_inputs(seed: int = 0) -> dict:
    seeds = jax.random.split(jax.random.key(seed), 11)
    return {
        "residual_in": scatter_about(seeds[0], (TOKENS, D), 1.0, 6.0, ((0, 64),)),
        "query_rows": draw_query_rows(jax.random.fold_in(seeds[10], 71), 0),
        "key_rows": draw_key_rows(jax.random.fold_in(seeds[10], 71), 0),
        "value_rows": draw_value_rows(jax.random.fold_in(seeds[10], 71), 0),
        "rand_blocks": draw_rand_blocks(jax.random.fold_in(seeds[10], 71), 0),
        "global_blocks": draw_global_blocks(jax.random.fold_in(seeds[10], 71), 0),
        "out_weight": scatter_about(seeds[6], (D, D), D ** -0.5, 0.1875, ((0, 2),)),
        "norm_gain": jnp.clip(1.0 + 0.15 * jax.random.normal(seeds[7], (D,), jnp.float32), 0.25, 1.75),
        "up_weight": scatter_about(seeds[8], (D, FF), D ** -0.5, 0.1875, ((1, 2),)),
        "down_weight": scatter_about(seeds[9], (FF, D), FF ** -0.5, 0.09375, ((0, 2),)),
    }


def reference(residual_in, query_rows, key_rows, value_rows, rand_blocks, global_blocks, out_weight, norm_gain, up_weight, down_weight):
    score_scale = 1.0 / math.sqrt(HD)
    segments = NB // QB_DEV

    def heads_first(array):
        return array.reshape(NB, BLK, H, HD).transpose(2, 0, 1, 3)
    q_heads = heads_first(query_rows)
    k_heads = heads_first(key_rows)
    v_heads = heads_first(value_rows)
    rand_heads = rand_blocks.transpose(1, 0, 2).astype(jnp.int32)
    block_ids = jnp.arange(NB, dtype=jnp.int32)
    window = jnp.stack([(block_ids - 1) % NB, block_ids, (block_ids + 1) % NB], axis=1)
    global_cols = jnp.broadcast_to(global_blocks.astype(jnp.int32)[None, :], (NB, GLOB))
    always_on = jnp.ones((NB, 1), dtype=bool)
    valid_cols = jnp.concatenate([(block_ids >= 1)[:, None], always_on, (block_ids + 1 < NB)[:, None], jnp.ones((NB, R + GLOB), dtype=bool)], axis=1)

    def sparse_head(inputs):
        q_one, k_one, v_one, rand_one = inputs
        chosen = jnp.concatenate([window, rand_one, global_cols], axis=1)
        k_sel = k_one[chosen].astype(jnp.float32)
        v_sel = v_one[chosen].astype(jnp.float32)
        scores = jnp.einsum('nqd,njkd->nqjk', q_one.astype(jnp.float32), k_sel) * score_scale
        scores = jnp.where(valid_cols[:, None, :, None], scores, jnp.float32(-1e+30))
        row_peak = lax.optimization_barrier(jnp.max(scores, axis=(2, 3), keepdims=True))
        weights = jnp.exp(scores - row_peak)
        row_total = lax.optimization_barrier(jnp.sum(weights, axis=(2, 3)))
        rounded = lax.optimization_barrier(weights.astype(jnp.bfloat16)).astype(jnp.float32)
        mixed_sum = jnp.einsum('nqjk,njkd->nqd', rounded, v_sel)
        return mixed_sum / row_total[..., None]
    sparse_out = lax.map(sparse_head, (q_heads, k_heads, v_heads, rand_heads))

    def global_head(inputs):
        q_one, k_one, v_one = inputs
        global_q = q_one[global_blocks.astype(jnp.int32)].reshape(GLOB * BLK, HD).astype(jnp.float32)
        k_segs = k_one.reshape(segments, TOK_DEV, HD)
        v_segs = v_one.reshape(segments, TOK_DEV, HD)

        def fold_segment(state_now, segment):
            best, summed, accum = state_now
            k_seg, v_seg = segment
            scores = jnp.dot(global_q, k_seg.astype(jnp.float32).T) * score_scale
            seg_peak = lax.optimization_barrier(jnp.max(scores, axis=1))
            weights = jnp.exp(scores - seg_peak[:, None])
            seg_total = lax.optimization_barrier(jnp.sum(weights, axis=1))
            rounded = lax.optimization_barrier(weights.astype(jnp.bfloat16)).astype(jnp.float32)
            seg_acc = jnp.dot(rounded, v_seg.astype(jnp.float32))
            larger = jnp.maximum(best, seg_peak)
            factor_old = jnp.exp(best - larger)
            factor_new = jnp.exp(seg_peak - larger)
            return ((larger, summed * factor_old + seg_total * factor_new, accum * factor_old[:, None] + seg_acc * factor_new[:, None]), None)
        start_state = (jnp.full((GLOB * BLK,), -1e+30, dtype=jnp.float32), jnp.zeros((GLOB * BLK,), jnp.float32), jnp.zeros((GLOB * BLK, HD), jnp.float32))
        final_state, _ = lax.scan(fold_segment, start_state, (k_segs, v_segs))
        return (final_state[2] / final_state[1][:, None]).reshape(GLOB, BLK, HD)
    global_out = lax.map(global_head, (q_heads, k_heads, v_heads))
    merged = sparse_out.at[:, global_blocks.astype(jnp.int32)].set(global_out)
    attention = merged.transpose(1, 2, 0, 3).reshape(TOKENS, D).astype(jnp.bfloat16)
    projected = jnp.dot(attention, out_weight, preferred_element_type=jnp.float32)
    middle = (residual_in.astype(jnp.float32) + projected).astype(jnp.bfloat16)
    middle32 = middle.astype(jnp.float32)
    row_mean = lax.optimization_barrier(jnp.mean(middle32, axis=1, keepdims=True))
    centered = middle32 - row_mean
    row_var = lax.optimization_barrier(jnp.mean(centered * centered, axis=1, keepdims=True))
    normed = (centered * lax.rsqrt(row_var + 1e-05) * norm_gain).astype(jnp.bfloat16)
    hidden = jax.nn.gelu(jnp.dot(normed, up_weight, preferred_element_type=jnp.float32), approximate=True).astype(jnp.bfloat16)
    down_out = jnp.dot(hidden, down_weight, preferred_element_type=jnp.float32)
    return (middle32 + down_out).astype(jnp.bfloat16)
```

```python
import math

import jax
import jax.numpy as jnp
from jax import lax
from jax.sharding import PartitionSpec as P

HD = 64
BLK = 64
R = 3
GLOB = 2
GROUP = 16
QB_DEV = 16


def with_halo(block, sides, width):
    for axis, dim in sides:
        count = lax.axis_size(axis)
        forward = [(i, i + 1) for i in range(count - 1)]
        backward = [(target, source) for source, target in forward]
        low = lax.ppermute(
            lax.slice_in_dim(block, block.shape[dim] - width, None, axis=dim), axis, forward
        )
        high = lax.ppermute(lax.slice_in_dim(block, 0, width, axis=dim), axis, backward)
        block = jnp.concatenate([low, block, high], axis=dim)
    return block


def swapped(block, axis, apart):
    count = lax.axis_size(axis)
    route = []
    for low in range(count):
        high = low | 1 << apart
        if high != low and high < count:
            route += [(low, high), (high, low)]
    return lax.ppermute(block, axis, route)


def tree_sum(block, axis):
    for bit in range(lax.axis_size(axis).bit_length() - 1):
        block = block + swapped(block, axis, bit)
    return block


def merge_packed(first, second):
    larger = jnp.maximum(first[..., :1], second[..., :1])
    mixed = first[..., 1:] * jnp.exp(first[..., :1] - larger) + second[..., 1:] * jnp.exp(
        second[..., :1] - larger
    )
    return jnp.concatenate([larger, mixed], axis=-1)


def tree_merge(packed, axis):
    for bit in range(lax.axis_size(axis).bit_length() - 1):
        packed = merge_packed(packed, swapped(packed, axis, bit))
    return packed


def joined(shard, axis, combine):
    everything = jax.tree.map(lambda part: lax.all_gather(part, axis), shard)
    initial = jax.tree.map(lambda part: part[0], everything)

    def hop(k, so_far):
        return combine(so_far, jax.tree.map(lambda part: part[k], everything))

    return lax.fori_loop(1, lax.axis_size(axis), hop, initial)


def combine_parts(first_part, second_part):
    peak_a, total_a, accum_a = first_part
    peak_b, total_b, accum_b = second_part
    larger = jnp.maximum(peak_a, peak_b)
    factor_a = jnp.exp(peak_a - larger)
    factor_b = jnp.exp(peak_b - larger)
    return (
        larger,
        total_a * factor_a + total_b * factor_b,
        accum_a * factor_a[..., None] + accum_b * factor_b[..., None],
    )


def local(
    residual_in,
    query_rows,
    key_rows,
    value_rows,
    rand_blocks,
    global_blocks,
    out_weight,
    norm_gain,
    up_weight,
    down_weight,
):
    tok_rows = query_rows.shape[0]
    local_width = query_rows.shape[1]
    heads_here = local_width // HD
    shard_count = lax.axis_size("seq")
    my_shard = lax.axis_index("seq")
    total_blocks = QB_DEV * shard_count
    score_scale = 1.0 / math.sqrt(HD)
    q_heads = query_rows.reshape(QB_DEV, BLK, heads_here, HD)
    key_heads = key_rows.reshape(tok_rows, heads_here, HD)
    value_heads = value_rows.reshape(tok_rows, heads_here, HD)
    kv_tokens = jnp.concatenate([key_heads, value_heads], axis=2)
    padded = with_halo(kv_tokens, (("seq", 0),), BLK)
    padded_blocks = padded.reshape(QB_DEV + 2, BLK, heads_here, 2 * HD).transpose(0, 2, 1, 3)
    own_blocks = padded_blocks[1:-1]
    window_kv = jnp.stack([padded_blocks[:-2], own_blocks, padded_blocks[2:]], axis=2)
    flat_kv = own_blocks.reshape(QB_DEV * heads_here, BLK, 2 * HD)
    position = my_shard % GROUP
    group_base = my_shard - position
    slot_count = QB_DEV * heads_here * R
    capacity = slot_count // GROUP
    offsets_all = jnp.arange(GROUP, dtype=jnp.int32)
    slot_heads = jnp.arange(slot_count, dtype=jnp.int32) // R % heads_here
    cap_range = jnp.arange(capacity, dtype=jnp.int32)

    def requests_of(shard):
        request_rows = lax.dynamic_slice_in_dim(rand_blocks, shard * QB_DEV, QB_DEV, 0)
        return request_rows.reshape(slot_count)

    def payload_for(offset):
        requester = group_base + (position - offset) % GROUP
        wanted = requests_of(requester)
        from_me = wanted // QB_DEV == my_shard
        order_rank = jnp.cumsum(from_me.astype(jnp.int32)) - 1
        source = wanted % QB_DEV * heads_here + slot_heads
        pick_table = from_me[:, None] & (order_rank[:, None] == cap_range[None, :])
        chosen = jnp.sum(jnp.where(pick_table, source[:, None], 0), axis=0)
        return jnp.take(flat_kv, chosen, axis=0)

    my_requests = requests_of(my_shard)
    owner_offset = (my_requests // QB_DEV - group_base - position) % GROUP
    offset_hits = owner_offset[:, None] == offsets_all[None, :]
    rank_table = jnp.cumsum(offset_hits.astype(jnp.int32), axis=0) - 1
    my_rank = jnp.sum(jnp.where(offset_hits, rank_table, 0), axis=1)
    slot_index = owner_offset * capacity + my_rank
    sectioned = jax.vmap(payload_for)(offsets_all)
    shard_ids = range(shard_count)
    arrived = [sectioned[0]]
    for offset in range(1, GROUP):
        route = [(s, s - s % GROUP + (s % GROUP - offset) % GROUP) for s in shard_ids]
        arrived.append(lax.ppermute(sectioned[offset], "seq", route))
    received = jnp.stack(arrived, axis=0)
    random_kv = jnp.take(received.reshape(GROUP * capacity, BLK, 2 * HD), slot_index, axis=0)
    random_kv = random_kv.reshape(QB_DEV, heads_here, R, BLK, 2 * HD)
    packed = jnp.stack([query_rows, key_rows, value_rows], axis=0)
    contributions = []
    for which in range(GLOB):
        global_id = global_blocks[which]
        block_rows = lax.dynamic_slice_in_dim(packed, global_id % QB_DEV * BLK, BLK, 1)
        is_owner = global_id // QB_DEV == my_shard
        contributions.append(jnp.where(is_owner, block_rows, jnp.zeros_like(block_rows)))
    global_packed = tree_sum(jnp.stack(contributions, axis=0), "seq")
    global_q = global_packed[:, 0].reshape(GLOB, BLK, heads_here, HD)
    global_k = global_packed[:, 1].reshape(GLOB, BLK, heads_here, HD)
    global_v = global_packed[:, 2].reshape(GLOB, BLK, heads_here, HD)
    global_kv = jnp.concatenate([global_k, global_v], axis=3).transpose(2, 0, 1, 3)
    global_kv = jnp.broadcast_to(global_kv[None], (QB_DEV, heads_here, GLOB, BLK, 2 * HD))
    all_kv = jnp.concatenate([window_kv, random_kv, global_kv], axis=2)
    keys_all = all_kv[..., :HD]
    values_all = all_kv[..., HD:]
    scores = (
        jnp.einsum("bqhd,bhjkd->bhqjk", q_heads, keys_all, preferred_element_type=jnp.float32)
        * score_scale
    )
    block_global = my_shard * QB_DEV + jnp.arange(QB_DEV, dtype=jnp.int32)
    valid_cols = jnp.concatenate(
        [
            (block_global >= 1)[:, None],
            jnp.ones((QB_DEV, 1), dtype=bool),
            (block_global + 1 < total_blocks)[:, None],
            jnp.ones((QB_DEV, R + GLOB), dtype=bool),
        ],
        axis=1,
    )
    scores = jnp.where(valid_cols[:, None, None, :, None], scores, jnp.float32(-1e30))
    row_peak = jnp.max(scores, axis=(3, 4), keepdims=True)
    weights = jnp.exp(scores - row_peak)
    row_total = jnp.sum(weights, axis=(3, 4))
    mixed_sum = jnp.einsum(
        "bhqjk,bhjkd->bqhd",
        weights.astype(jnp.bfloat16),
        values_all,
        preferred_element_type=jnp.float32,
    )
    sparse_out = mixed_sum / row_total.transpose(0, 2, 1)[..., None]
    global_scores = (
        jnp.einsum("gqhd,thd->ghqt", global_q, key_heads, preferred_element_type=jnp.float32)
        * score_scale
    )
    seg_peak = jnp.max(global_scores, axis=3)
    seg_weights = jnp.exp(global_scores - seg_peak[..., None])
    seg_total = jnp.sum(seg_weights, axis=3)
    seg_acc = jnp.einsum(
        "ghqt,thd->ghqd",
        seg_weights.astype(jnp.bfloat16),
        value_heads,
        preferred_element_type=jnp.float32,
    )
    merged = tree_merge(
        jnp.concatenate([seg_peak[..., None], seg_total[..., None], seg_acc], axis=-1), "seq"
    )
    global_out = merged[..., 2:] / merged[..., 1:2]
    attn_rows = sparse_out.reshape(tok_rows, local_width)
    for which in range(GLOB):
        global_id = global_blocks[which]
        start_row = global_id % QB_DEV * BLK
        current = lax.dynamic_slice_in_dim(attn_rows, start_row, BLK, 0)
        replacing = global_out[which].transpose(1, 0, 2).reshape(BLK, local_width)
        is_owner = global_id // QB_DEV == my_shard
        attn_rows = lax.dynamic_update_slice_in_dim(
            attn_rows, jnp.where(is_owner, replacing, current), start_row, 0
        )
    attention = attn_rows.astype(jnp.bfloat16)
    mp_index = lax.axis_index("mp")
    mp_route = [(0, 1), (1, 0)]
    half_width = residual_in.shape[1] // lax.axis_size("mp")
    other_attention = lax.ppermute(attention, "mp", mp_route)
    other_weight = lax.ppermute(out_weight, "mp", mp_route)
    projected = jnp.dot(attention, out_weight, preferred_element_type=jnp.float32) + jnp.dot(
        other_attention, other_weight, preferred_element_type=jnp.float32
    )
    middle = (residual_in.astype(jnp.float32) + projected).astype(jnp.bfloat16)
    middle_own = lax.dynamic_slice_in_dim(middle, mp_index * half_width, half_width, 1)
    middle32 = middle.astype(jnp.float32)
    row_mean = jnp.mean(middle32, axis=1, keepdims=True)
    centered = middle32 - row_mean
    row_var = jnp.mean(centered * centered, axis=1, keepdims=True)
    normed = (centered * lax.rsqrt(row_var + 1e-05) * norm_gain).astype(jnp.bfloat16)
    hidden = jax.nn.gelu(
        jnp.dot(normed, up_weight, preferred_element_type=jnp.float32), approximate=True
    ).astype(jnp.bfloat16)
    weight_mine = lax.dynamic_slice_in_dim(down_weight, mp_index * half_width, half_width, 1)
    weight_other = lax.dynamic_slice_in_dim(down_weight, (1 - mp_index) * half_width, half_width, 1)
    for_other = jnp.dot(hidden, weight_other, preferred_element_type=jnp.float32)
    from_other = lax.ppermute(for_other, "mp", mp_route)
    down_mine = jnp.dot(hidden, weight_mine, preferred_element_type=jnp.float32)
    return (middle_own.astype(jnp.float32) + (down_mine + from_other)).astype(jnp.bfloat16)


def solution(mesh):
    placed = (
        P("seq", None),
        P("seq", "mp"),
        P("seq", "mp"),
        P("seq", "mp"),
        P(None, "mp", None),
        P(),
        P("mp", None),
        P(),
        P(None, "mp"),
        P("mp", None),
    )
    return jax.shard_map(
        local, mesh=mesh, in_specs=placed, out_specs=P("seq", "mp"), check_vma=False
    )
```

```python
import math

import jax
import jax.numpy as jnp
from jax import lax
from jax.sharding import PartitionSpec as P

HD = 64
BLK = 64
R = 3
GLOB = 2
GROUP = 16
QB_DEV = 16


def with_halo(block, sides, width):
    for axis, dim in sides:
        count = lax.axis_size(axis)
        forward = [(i, i + 1) for i in range(count - 1)]
        backward = [(target, source) for source, target in forward]
        low = lax.ppermute(
            lax.slice_in_dim(block, block.shape[dim] - width, None, axis=dim), axis, forward
        )
        high = lax.ppermute(lax.slice_in_dim(block, 0, width, axis=dim), axis, backward)
        block = jnp.concatenate([low, block, high], axis=dim)
    return block


def swapped(block, axis, apart):
    count = lax.axis_size(axis)
    route = []
    for low in range(count):
        high = low | 1 << apart
        if high != low and high < count:
            route += [(low, high), (high, low)]
    return lax.ppermute(block, axis, route)


def xor_partners(block, axis, low_bit, width):
    count = lax.axis_size(axis)
    return [
        lax.ppermute(block, axis, [(i, i ^ k << low_bit) for i in range(count)])
        for k in range(1, 1 << width)
    ]


def tree_stages(axis):
    bits = lax.axis_size(axis).bit_length() - 1
    return [(low, min(2, bits - low)) for low in range(0, bits, 2)]


def tree_sum(block, axis):
    for low_bit, width in tree_stages(axis):
        for part in xor_partners(block, axis, low_bit, width):
            block = block + part
    return block


def merge_packed(parts):
    larger = parts[0][..., :1]
    for part in parts[1:]:
        larger = jnp.maximum(larger, part[..., :1])
    mixed = parts[0][..., 1:] * jnp.exp(parts[0][..., :1] - larger)
    for part in parts[1:]:
        mixed = mixed + part[..., 1:] * jnp.exp(part[..., :1] - larger)
    return jnp.concatenate([larger, mixed], axis=-1)


def tree_merge(packed, axis):
    for low_bit, width in tree_stages(axis):
        packed = merge_packed([packed] + xor_partners(packed, axis, low_bit, width))
    return packed


def local(
    residual_in,
    query_rows,
    key_rows,
    value_rows,
    rand_blocks,
    global_blocks,
    out_weight,
    norm_gain,
    up_weight,
    down_weight,
):
    tok_rows = query_rows.shape[0]
    local_width = query_rows.shape[1]
    heads_here = local_width // HD
    shard_count = lax.axis_size("seq")
    my_shard = lax.axis_index("seq")
    total_blocks = QB_DEV * shard_count
    score_scale = 1.0 / math.sqrt(HD)
    q_heads = query_rows.reshape(QB_DEV, BLK, heads_here, HD)
    key_heads = key_rows.reshape(tok_rows, heads_here, HD)
    value_heads = value_rows.reshape(tok_rows, heads_here, HD)
    kv_tokens = jnp.concatenate([key_heads, value_heads], axis=2)
    padded = with_halo(kv_tokens, (("seq", 0),), BLK)
    padded_blocks = padded.reshape(QB_DEV + 2, BLK, heads_here, 2 * HD).transpose(0, 2, 1, 3)
    own_blocks = padded_blocks[1:-1]
    window_kv = jnp.stack([padded_blocks[:-2], own_blocks, padded_blocks[2:]], axis=2)
    flat_kv = own_blocks.reshape(QB_DEV * heads_here, BLK, 2 * HD)
    position = my_shard % GROUP
    group_base = my_shard - position
    slot_count = QB_DEV * heads_here * R
    capacity = slot_count // GROUP
    offsets_all = jnp.arange(GROUP, dtype=jnp.int32)
    slot_heads = jnp.arange(slot_count, dtype=jnp.int32) // R % heads_here
    cap_range = jnp.arange(capacity, dtype=jnp.int32)

    def requests_of(shard):
        request_rows = lax.dynamic_slice_in_dim(rand_blocks, shard * QB_DEV, QB_DEV, 0)
        return request_rows.reshape(slot_count)

    def payload_for(offset):
        requester = group_base + (position - offset) % GROUP
        wanted = requests_of(requester)
        from_me = wanted // QB_DEV == my_shard
        order_rank = jnp.cumsum(from_me.astype(jnp.int32)) - 1
        source = wanted % QB_DEV * heads_here + slot_heads
        pick_table = from_me[:, None] & (order_rank[:, None] == cap_range[None, :])
        chosen = jnp.sum(jnp.where(pick_table, source[:, None], 0), axis=0)
        return jnp.take(flat_kv, chosen, axis=0)

    my_requests = requests_of(my_shard)
    owner_offset = (my_requests // QB_DEV - group_base - position) % GROUP
    offset_hits = owner_offset[:, None] == offsets_all[None, :]
    rank_table = jnp.cumsum(offset_hits.astype(jnp.int32), axis=0) - 1
    my_rank = jnp.sum(jnp.where(offset_hits, rank_table, 0), axis=1)
    slot_index = owner_offset * capacity + my_rank
    sectioned = jax.vmap(payload_for)(offsets_all)
    shard_ids = range(shard_count)
    arrived = [sectioned[0]]
    for offset in range(1, GROUP):
        route = [(s, s - s % GROUP + (s % GROUP - offset) % GROUP) for s in shard_ids]
        arrived.append(lax.ppermute(sectioned[offset], "seq", route))
    received = jnp.stack(arrived, axis=0)
    random_kv = jnp.take(received.reshape(GROUP * capacity, BLK, 2 * HD), slot_index, axis=0)
    random_kv = random_kv.reshape(QB_DEV, heads_here, R, BLK, 2 * HD)
    packed = jnp.stack([query_rows, key_rows, value_rows], axis=0)
    contributions = []
    for which in range(GLOB):
        global_id = global_blocks[which]
        block_rows = lax.dynamic_slice_in_dim(packed, global_id % QB_DEV * BLK, BLK, 1)
        is_owner = global_id // QB_DEV == my_shard
        contributions.append(jnp.where(is_owner, block_rows, jnp.zeros_like(block_rows)))
    global_packed = tree_sum(jnp.stack(contributions, axis=0), "seq")
    global_q = global_packed[:, 0].reshape(GLOB, BLK, heads_here, HD)
    global_k = global_packed[:, 1].reshape(GLOB, BLK, heads_here, HD)
    global_v = global_packed[:, 2].reshape(GLOB, BLK, heads_here, HD)
    global_kv = jnp.concatenate([global_k, global_v], axis=3).transpose(2, 0, 1, 3)
    global_kv = jnp.broadcast_to(global_kv[None], (QB_DEV, heads_here, GLOB, BLK, 2 * HD))
    all_kv = jnp.concatenate([window_kv, random_kv, global_kv], axis=2)
    keys_all = all_kv[..., :HD]
    values_all = all_kv[..., HD:]
    scores = (
        jnp.einsum("bqhd,bhjkd->bhqjk", q_heads, keys_all, preferred_element_type=jnp.float32)
        * score_scale
    )
    block_global = my_shard * QB_DEV + jnp.arange(QB_DEV, dtype=jnp.int32)
    valid_cols = jnp.concatenate(
        [
            (block_global >= 1)[:, None],
            jnp.ones((QB_DEV, 1), dtype=bool),
            (block_global + 1 < total_blocks)[:, None],
            jnp.ones((QB_DEV, R + GLOB), dtype=bool),
        ],
        axis=1,
    )
    scores = jnp.where(valid_cols[:, None, None, :, None], scores, jnp.float32(-1e30))
    row_peak = jnp.max(scores, axis=(3, 4), keepdims=True)
    weights = jnp.exp(scores - row_peak)
    row_total = jnp.sum(weights, axis=(3, 4))
    mixed_sum = jnp.einsum(
        "bhqjk,bhjkd->bqhd",
        weights.astype(jnp.bfloat16),
        values_all,
        preferred_element_type=jnp.float32,
    )
    sparse_out = mixed_sum / row_total.transpose(0, 2, 1)[..., None]
    global_scores = (
        jnp.einsum("gqhd,thd->ghqt", global_q, key_heads, preferred_element_type=jnp.float32)
        * score_scale
    )
    seg_peak = jnp.max(global_scores, axis=3)
    seg_weights = jnp.exp(global_scores - seg_peak[..., None])
    seg_total = jnp.sum(seg_weights, axis=3)
    seg_acc = jnp.einsum(
        "ghqt,thd->ghqd",
        seg_weights.astype(jnp.bfloat16),
        value_heads,
        preferred_element_type=jnp.float32,
    )
    mp_index = lax.axis_index("mp")
    mp_route = [(0, 1), (1, 0)]
    half_width = residual_in.shape[1] // lax.axis_size("mp")
    other_up = lax.ppermute(up_weight, "mp", mp_route)
    other_index = 1 - mp_index
    their_down = lax.dynamic_slice_in_dim(down_weight, other_index * half_width, half_width, 1)
    other_down = lax.ppermute(their_down, "mp", mp_route)
    seg_packed = jnp.concatenate([seg_peak[..., None], seg_total[..., None], seg_acc], axis=-1)
    seg_packed, other_up, other_down = lax.optimization_barrier((seg_packed, other_up, other_down))
    merged = tree_merge(seg_packed, "seq")
    global_out = merged[..., 2:] / merged[..., 1:2]
    attn_rows = sparse_out.reshape(tok_rows, local_width)
    for which in range(GLOB):
        global_id = global_blocks[which]
        start_row = global_id % QB_DEV * BLK
        current = lax.dynamic_slice_in_dim(attn_rows, start_row, BLK, 0)
        replacing = global_out[which].transpose(1, 0, 2).reshape(BLK, local_width)
        is_owner = global_id // QB_DEV == my_shard
        attn_rows = lax.dynamic_update_slice_in_dim(
            attn_rows, jnp.where(is_owner, replacing, current), start_row, 0
        )
    attention = attn_rows.astype(jnp.bfloat16)
    other_attention = lax.ppermute(attention, "mp", mp_route)
    other_weight = lax.ppermute(out_weight, "mp", mp_route)
    projected = jnp.dot(attention, out_weight, preferred_element_type=jnp.float32) + jnp.dot(
        other_attention, other_weight, preferred_element_type=jnp.float32
    )
    middle = (residual_in.astype(jnp.float32) + projected).astype(jnp.bfloat16)
    middle_own = lax.dynamic_slice_in_dim(middle, mp_index * half_width, half_width, 1)
    middle32 = middle.astype(jnp.float32)
    row_mean = jnp.mean(middle32, axis=1, keepdims=True)
    centered = middle32 - row_mean
    row_var = jnp.mean(centered * centered, axis=1, keepdims=True)
    normed = (centered * lax.rsqrt(row_var + 1e-05) * norm_gain).astype(jnp.bfloat16)
    own_down = lax.dynamic_slice_in_dim(down_weight, mp_index * half_width, half_width, 1)
    hidden_own = jax.nn.gelu(
        jnp.dot(normed, up_weight, preferred_element_type=jnp.float32), approximate=True
    ).astype(jnp.bfloat16)
    hidden_other = jax.nn.gelu(
        jnp.dot(normed, other_up, preferred_element_type=jnp.float32), approximate=True
    ).astype(jnp.bfloat16)
    down_part = jnp.dot(hidden_own, own_down, preferred_element_type=jnp.float32) + jnp.dot(
        hidden_other, other_down, preferred_element_type=jnp.float32
    )
    return (middle_own.astype(jnp.float32) + down_part).astype(jnp.bfloat16)


def solution(mesh):
    placed = (
        P("seq", None),
        P("seq", "mp"),
        P("seq", "mp"),
        P("seq", "mp"),
        P(None, "mp", None),
        P(),
        P("mp", None),
        P(),
        P(None, "mp"),
        P("mp", None),
    )
    return jax.shard_map(
        local, mesh=mesh, in_specs=placed, out_specs=P("seq", "mp"), check_vma=False
    )
```

```python
import math

import jax
import jax.numpy as jnp
from jax import lax
from jax.sharding import PartitionSpec as P

HD = 64
BLK = 64
R = 3
GLOB = 2
GROUP = 16
QB_DEV = 16
SEQ = ("seq_hi", "seq_lo")


def with_halo(block, sides, width):
    for axis, dim in sides:
        count = lax.axis_size(axis)
        forward = [(i, i + 1) for i in range(count - 1)]
        backward = [(target, source) for source, target in forward]
        low = lax.ppermute(
            lax.slice_in_dim(block, block.shape[dim] - width, None, axis=dim), axis, forward
        )
        high = lax.ppermute(lax.slice_in_dim(block, 0, width, axis=dim), axis, backward)
        block = jnp.concatenate([low, block, high], axis=dim)
    return block


def swapped(block, axis, apart):
    count = lax.axis_size(axis)
    route = []
    for low in range(count):
        high = low | 1 << apart
        if high != low and high < count:
            route += [(low, high), (high, low)]
    return lax.ppermute(block, axis, route)


def xor_partners(block, axis, low_bit, width):
    count = lax.axis_size(axis)
    return [
        lax.ppermute(block, axis, [(i, i ^ k << low_bit) for i in range(count)])
        for k in range(1, 1 << width)
    ]


def tree_stages(axis):
    bits = lax.axis_size(axis).bit_length() - 1
    return [(low, min(2, bits - low)) for low in range(0, bits, 2)]


def tree_sum(block, axis):
    for low_bit, width in tree_stages(axis):
        for part in xor_partners(block, axis, low_bit, width):
            block = block + part
    return block


def merge_packed(parts):
    larger = parts[0][..., :1]
    for part in parts[1:]:
        larger = jnp.maximum(larger, part[..., :1])
    mixed = parts[0][..., 1:] * jnp.exp(parts[0][..., :1] - larger)
    for part in parts[1:]:
        mixed = mixed + part[..., 1:] * jnp.exp(part[..., :1] - larger)
    return jnp.concatenate([larger, mixed], axis=-1)


def tree_merge(packed, axis):
    for low_bit, width in tree_stages(axis):
        packed = merge_packed([packed] + xor_partners(packed, axis, low_bit, width))
    return packed


def local(
    residual_in,
    query_rows,
    key_rows,
    value_rows,
    rand_blocks,
    global_blocks,
    out_weight,
    norm_gain,
    up_weight,
    down_weight,
):
    tok_rows = query_rows.shape[0]
    local_width = query_rows.shape[1]
    heads_here = local_width // HD
    shard_count = lax.axis_size(SEQ)
    my_shard = lax.axis_index(SEQ)
    total_blocks = QB_DEV * shard_count
    score_scale = 1.0 / math.sqrt(HD)
    q_heads = query_rows.reshape(QB_DEV, BLK, heads_here, HD)
    key_heads = key_rows.reshape(tok_rows, heads_here, HD)
    value_heads = value_rows.reshape(tok_rows, heads_here, HD)
    kv_tokens = jnp.concatenate([key_heads, value_heads], axis=2)
    padded = with_halo(kv_tokens, ((SEQ, 0),), BLK)
    padded_blocks = padded.reshape(QB_DEV + 2, BLK, heads_here, 2 * HD).transpose(0, 2, 1, 3)
    own_blocks = padded_blocks[1:-1]
    window_kv = jnp.stack([padded_blocks[:-2], own_blocks, padded_blocks[2:]], axis=2)
    flat_kv = own_blocks.reshape(QB_DEV * heads_here, BLK, 2 * HD)
    position = my_shard % GROUP
    group_base = my_shard - position
    slot_count = QB_DEV * heads_here * R
    capacity = slot_count // GROUP
    offsets_all = jnp.arange(GROUP, dtype=jnp.int32)
    slot_heads = jnp.arange(slot_count, dtype=jnp.int32) // R % heads_here
    cap_range = jnp.arange(capacity, dtype=jnp.int32)

    def requests_of(shard):
        request_rows = lax.dynamic_slice_in_dim(rand_blocks, shard * QB_DEV, QB_DEV, 0)
        return request_rows.reshape(slot_count)

    def payload_for(target):
        requester = group_base + target
        wanted = requests_of(requester)
        from_me = wanted // QB_DEV == my_shard
        order_rank = jnp.cumsum(from_me.astype(jnp.int32)) - 1
        source = wanted % QB_DEV * heads_here + slot_heads
        pick_table = from_me[:, None] & (order_rank[:, None] == cap_range[None, :])
        chosen = jnp.sum(jnp.where(pick_table, source[:, None], 0), axis=0)
        return jnp.take(flat_kv, chosen, axis=0)

    my_requests = requests_of(my_shard)
    owner_position = my_requests // QB_DEV - group_base
    offset_hits = owner_position[:, None] == offsets_all[None, :]
    rank_table = jnp.cumsum(offset_hits.astype(jnp.int32), axis=0) - 1
    my_rank = jnp.sum(jnp.where(offset_hits, rank_table, 0), axis=1)
    slot_index = owner_position * capacity + my_rank
    sectioned = jax.vmap(payload_for)(offsets_all)
    received = lax.all_to_all(
        sectioned.reshape(GROUP * capacity, BLK, 2 * HD), "seq_lo", 0, 0, tiled=True
    )
    random_kv = jnp.take(received, slot_index, axis=0)
    random_kv = random_kv.reshape(QB_DEV, heads_here, R, BLK, 2 * HD)
    packed = jnp.stack([query_rows, key_rows, value_rows], axis=0)
    contributions = []
    for which in range(GLOB):
        global_id = global_blocks[which]
        block_rows = lax.dynamic_slice_in_dim(packed, global_id % QB_DEV * BLK, BLK, 1)
        is_owner = global_id // QB_DEV == my_shard
        contributions.append(jnp.where(is_owner, block_rows, jnp.zeros_like(block_rows)))
    global_packed = tree_sum(jnp.stack(contributions, axis=0), SEQ)
    global_q = global_packed[:, 0].reshape(GLOB, BLK, heads_here, HD)
    global_k = global_packed[:, 1].reshape(GLOB, BLK, heads_here, HD)
    global_v = global_packed[:, 2].reshape(GLOB, BLK, heads_here, HD)
    global_kv = jnp.concatenate([global_k, global_v], axis=3).transpose(2, 0, 1, 3)
    global_kv = jnp.broadcast_to(global_kv[None], (QB_DEV, heads_here, GLOB, BLK, 2 * HD))
    all_kv = jnp.concatenate([window_kv, random_kv, global_kv], axis=2)
    keys_all = all_kv[..., :HD]
    values_all = all_kv[..., HD:]
    scores = (
        jnp.einsum("bqhd,bhjkd->bhqjk", q_heads, keys_all, preferred_element_type=jnp.float32)
        * score_scale
    )
    block_global = my_shard * QB_DEV + jnp.arange(QB_DEV, dtype=jnp.int32)
    valid_cols = jnp.concatenate(
        [
            (block_global >= 1)[:, None],
            jnp.ones((QB_DEV, 1), dtype=bool),
            (block_global + 1 < total_blocks)[:, None],
            jnp.ones((QB_DEV, R + GLOB), dtype=bool),
        ],
        axis=1,
    )
    scores = jnp.where(valid_cols[:, None, None, :, None], scores, jnp.float32(-1e30))
    row_peak = jnp.max(scores, axis=(3, 4), keepdims=True)
    weights = jnp.exp(scores - row_peak)
    row_total = jnp.sum(weights, axis=(3, 4))
    mixed_sum = jnp.einsum(
        "bhqjk,bhjkd->bqhd",
        weights.astype(jnp.bfloat16),
        values_all,
        preferred_element_type=jnp.float32,
    )
    sparse_out = mixed_sum / row_total.transpose(0, 2, 1)[..., None]
    global_scores = (
        jnp.einsum("gqhd,thd->ghqt", global_q, key_heads, preferred_element_type=jnp.float32)
        * score_scale
    )
    seg_peak = jnp.max(global_scores, axis=3)
    seg_weights = jnp.exp(global_scores - seg_peak[..., None])
    seg_total = jnp.sum(seg_weights, axis=3)
    seg_acc = jnp.einsum(
        "ghqt,thd->ghqd",
        seg_weights.astype(jnp.bfloat16),
        value_heads,
        preferred_element_type=jnp.float32,
    )
    mp_index = lax.axis_index("mp")
    mp_route = [(0, 1), (1, 0)]
    half_width = residual_in.shape[1] // lax.axis_size("mp")
    other_up = lax.ppermute(up_weight, "mp", mp_route)
    other_index = 1 - mp_index
    their_down = lax.dynamic_slice_in_dim(down_weight, other_index * half_width, half_width, 1)
    other_down = lax.ppermute(their_down, "mp", mp_route)
    seg_packed = jnp.concatenate([seg_peak[..., None], seg_total[..., None], seg_acc], axis=-1)
    seg_packed, other_up, other_down = lax.optimization_barrier((seg_packed, other_up, other_down))
    merged = tree_merge(seg_packed, SEQ)
    global_out = merged[..., 2:] / merged[..., 1:2]
    attn_rows = sparse_out.reshape(tok_rows, local_width)
    for which in range(GLOB):
        global_id = global_blocks[which]
        start_row = global_id % QB_DEV * BLK
        current = lax.dynamic_slice_in_dim(attn_rows, start_row, BLK, 0)
        replacing = global_out[which].transpose(1, 0, 2).reshape(BLK, local_width)
        is_owner = global_id // QB_DEV == my_shard
        attn_rows = lax.dynamic_update_slice_in_dim(
            attn_rows, jnp.where(is_owner, replacing, current), start_row, 0
        )
    attention = attn_rows.astype(jnp.bfloat16)
    other_attention = lax.ppermute(attention, "mp", mp_route)
    other_weight = lax.ppermute(out_weight, "mp", mp_route)
    projected = jnp.dot(attention, out_weight, preferred_element_type=jnp.float32) + jnp.dot(
        other_attention, other_weight, preferred_element_type=jnp.float32
    )
    middle = (residual_in.astype(jnp.float32) + projected).astype(jnp.bfloat16)
    middle_own = lax.dynamic_slice_in_dim(middle, mp_index * half_width, half_width, 1)
    middle32 = middle.astype(jnp.float32)
    row_mean = jnp.mean(middle32, axis=1, keepdims=True)
    centered = middle32 - row_mean
    row_var = jnp.mean(centered * centered, axis=1, keepdims=True)
    normed = (centered * lax.rsqrt(row_var + 1e-05) * norm_gain).astype(jnp.bfloat16)
    own_down = lax.dynamic_slice_in_dim(down_weight, mp_index * half_width, half_width, 1)
    hidden_own = jax.nn.gelu(
        jnp.dot(normed, up_weight, preferred_element_type=jnp.float32), approximate=True
    ).astype(jnp.bfloat16)
    hidden_other = jax.nn.gelu(
        jnp.dot(normed, other_up, preferred_element_type=jnp.float32), approximate=True
    ).astype(jnp.bfloat16)
    down_part = jnp.dot(hidden_own, own_down, preferred_element_type=jnp.float32) + jnp.dot(
        hidden_other, other_down, preferred_element_type=jnp.float32
    )
    return (middle_own.astype(jnp.float32) + down_part).astype(jnp.bfloat16)


def solution(mesh):
    placed = (
        P(SEQ, None),
        P(SEQ, "mp"),
        P(SEQ, "mp"),
        P(SEQ, "mp"),
        P(None, "mp", None),
        P(),
        P("mp", None),
        P(),
        P(None, "mp"),
        P("mp", None),
    )
    seq_count = mesh.shape["seq"]
    split_mesh = jax.sharding.Mesh(
        mesh.devices.reshape(seq_count // GROUP, GROUP, mesh.shape["mp"]), SEQ + ("mp",)
    )
    return jax.shard_map(
        local, mesh=split_mesh, in_specs=placed, out_specs=P(SEQ, "mp"), check_vma=False
    )
```

```python
import math

import jax
import jax.numpy as jnp
from jax import lax
from jax.sharding import PartitionSpec as P

HD = 64
BLK = 64
R = 3
GLOB = 2
GROUP = 16
QB_DEV = 16


def with_halo(block, sides, width):
    for axis, dim in sides:
        count = lax.axis_size(axis)
        forward = [(i, i + 1) for i in range(count - 1)]
        backward = [(target, source) for source, target in forward]
        low = lax.ppermute(
            lax.slice_in_dim(block, block.shape[dim] - width, None, axis=dim), axis, forward
        )
        high = lax.ppermute(lax.slice_in_dim(block, 0, width, axis=dim), axis, backward)
        block = jnp.concatenate([low, block, high], axis=dim)
    return block


def swapped(block, axis, apart):
    count = lax.axis_size(axis)
    route = []
    for low in range(count):
        high = low | 1 << apart
        if high != low and high < count:
            route += [(low, high), (high, low)]
    return lax.ppermute(block, axis, route)


def xor_partners(block, axis, low_bit, width):
    count = lax.axis_size(axis)
    return [
        lax.ppermute(block, axis, [(i, i ^ k << low_bit) for i in range(count)])
        for k in range(1, 1 << width)
    ]


def tree_stages(axis):
    bits = lax.axis_size(axis).bit_length() - 1
    return [(low, min(2, bits - low)) for low in range(0, bits, 2)]


def tree_sum(block, axis):
    for low_bit, width in tree_stages(axis):
        for part in xor_partners(block, axis, low_bit, width):
            block = block + part
    return block


def merge_packed(parts):
    larger = parts[0][..., :1]
    for part in parts[1:]:
        larger = jnp.maximum(larger, part[..., :1])
    mixed = parts[0][..., 1:] * jnp.exp(parts[0][..., :1] - larger)
    for part in parts[1:]:
        mixed = mixed + part[..., 1:] * jnp.exp(part[..., :1] - larger)
    return jnp.concatenate([larger, mixed], axis=-1)


def tree_merge(packed, axis):
    for low_bit, width in tree_stages(axis):
        packed = merge_packed([packed] + xor_partners(packed, axis, low_bit, width))
    return packed


def local(
    residual_in,
    query_rows,
    key_rows,
    value_rows,
    rand_blocks,
    global_blocks,
    out_weight,
    norm_gain,
    up_weight,
    down_weight,
):
    tok_rows = query_rows.shape[0]
    local_width = query_rows.shape[1]
    heads_here = local_width // HD
    shard_count = lax.axis_size("seq")
    my_shard = lax.axis_index("seq")
    total_blocks = QB_DEV * shard_count
    score_scale = 1.0 / math.sqrt(HD)
    q_heads = query_rows.reshape(QB_DEV, BLK, heads_here, HD)
    key_heads = key_rows.reshape(tok_rows, heads_here, HD)
    value_heads = value_rows.reshape(tok_rows, heads_here, HD)
    kv_tokens = jnp.concatenate([key_heads, value_heads], axis=2)
    padded = with_halo(kv_tokens, (("seq", 0),), BLK)
    padded_blocks = padded.reshape(QB_DEV + 2, BLK, heads_here, 2 * HD).transpose(0, 2, 1, 3)
    own_blocks = padded_blocks[1:-1]
    window_kv = jnp.stack([padded_blocks[:-2], own_blocks, padded_blocks[2:]], axis=2)
    flat_kv = own_blocks.reshape(QB_DEV * heads_here, BLK, 2 * HD)
    position = my_shard % GROUP
    group_base = my_shard - position
    slot_count = QB_DEV * heads_here * R
    capacity = slot_count // GROUP
    offsets_all = jnp.arange(GROUP, dtype=jnp.int32)
    slot_heads = jnp.arange(slot_count, dtype=jnp.int32) // R % heads_here
    cap_range = jnp.arange(capacity, dtype=jnp.int32)

    def requests_of(shard):
        request_rows = lax.dynamic_slice_in_dim(rand_blocks, shard * QB_DEV, QB_DEV, 0)
        return request_rows.reshape(slot_count)

    def payload_for(offset):
        requester = group_base + (position - offset) % GROUP
        wanted = requests_of(requester)
        from_me = wanted // QB_DEV == my_shard
        order_rank = jnp.cumsum(from_me.astype(jnp.int32)) - 1
        source = wanted % QB_DEV * heads_here + slot_heads
        pick_table = from_me[:, None] & (order_rank[:, None] == cap_range[None, :])
        chosen = jnp.sum(jnp.where(pick_table, source[:, None], 0), axis=0)
        return jnp.take(flat_kv, chosen, axis=0)

    my_requests = requests_of(my_shard)
    owner_offset = (my_requests // QB_DEV - group_base - position) % GROUP
    offset_hits = owner_offset[:, None] == offsets_all[None, :]
    rank_table = jnp.cumsum(offset_hits.astype(jnp.int32), axis=0) - 1
    my_rank = jnp.sum(jnp.where(offset_hits, rank_table, 0), axis=1)
    slot_index = owner_offset * capacity + my_rank
    sectioned = jax.vmap(payload_for)(offsets_all)
    packed = jnp.stack([query_rows, key_rows, value_rows], axis=0)
    contributions = []
    for which in range(GLOB):
        global_id = global_blocks[which]
        block_rows = lax.dynamic_slice_in_dim(packed, global_id % QB_DEV * BLK, BLK, 1)
        is_owner = global_id // QB_DEV == my_shard
        contributions.append(jnp.where(is_owner, block_rows, jnp.zeros_like(block_rows)))

    global_packed = tree_sum(jnp.stack(contributions, axis=0), "seq")
    sectioned, global_packed = lax.optimization_barrier((sectioned, global_packed))
    shard_ids = range(shard_count)
    arrived = [sectioned[0]]
    for offset in range(1, GROUP):
        route = [(s, s - s % GROUP + (s % GROUP - offset) % GROUP) for s in shard_ids]
        arrived.append(lax.ppermute(sectioned[offset], "seq", route))
    received = jnp.stack(arrived, axis=0)
    random_kv = jnp.take(received.reshape(GROUP * capacity, BLK, 2 * HD), slot_index, axis=0)
    random_kv = random_kv.reshape(QB_DEV, heads_here, R, BLK, 2 * HD)
    global_q = global_packed[:, 0].reshape(GLOB, BLK, heads_here, HD)
    global_k = global_packed[:, 1].reshape(GLOB, BLK, heads_here, HD)
    global_v = global_packed[:, 2].reshape(GLOB, BLK, heads_here, HD)
    global_kv = jnp.concatenate([global_k, global_v], axis=3).transpose(2, 0, 1, 3)
    global_kv = jnp.broadcast_to(global_kv[None], (QB_DEV, heads_here, GLOB, BLK, 2 * HD))
    all_kv = jnp.concatenate([window_kv, random_kv, global_kv], axis=2)
    keys_all = all_kv[..., :HD]
    values_all = all_kv[..., HD:]
    scores = (
        jnp.einsum("bqhd,bhjkd->bhqjk", q_heads, keys_all, preferred_element_type=jnp.float32)
        * score_scale
    )
    block_global = my_shard * QB_DEV + jnp.arange(QB_DEV, dtype=jnp.int32)
    valid_cols = jnp.concatenate(
        [
            (block_global >= 1)[:, None],
            jnp.ones((QB_DEV, 1), dtype=bool),
            (block_global + 1 < total_blocks)[:, None],
            jnp.ones((QB_DEV, R + GLOB), dtype=bool),
        ],
        axis=1,
    )
    scores = jnp.where(valid_cols[:, None, None, :, None], scores, jnp.float32(-1e30))
    row_peak = jnp.max(scores, axis=(3, 4), keepdims=True)
    weights = jnp.exp(scores - row_peak)
    row_total = jnp.sum(weights, axis=(3, 4))
    mixed_sum = jnp.einsum(
        "bhqjk,bhjkd->bqhd",
        weights.astype(jnp.bfloat16),
        values_all,
        preferred_element_type=jnp.float32,
    )
    sparse_out = mixed_sum / row_total.transpose(0, 2, 1)[..., None]
    global_scores = (
        jnp.einsum("gqhd,thd->ghqt", global_q, key_heads, preferred_element_type=jnp.float32)
        * score_scale
    )
    seg_peak = jnp.max(global_scores, axis=3)
    seg_weights = jnp.exp(global_scores - seg_peak[..., None])
    seg_total = jnp.sum(seg_weights, axis=3)
    seg_acc = jnp.einsum(
        "ghqt,thd->ghqd",
        seg_weights.astype(jnp.bfloat16),
        value_heads,
        preferred_element_type=jnp.float32,
    )
    mp_index = lax.axis_index("mp")
    mp_route = [(0, 1), (1, 0)]
    half_width = residual_in.shape[1] // lax.axis_size("mp")
    other_up = lax.ppermute(up_weight, "mp", mp_route)
    other_index = 1 - mp_index
    their_down = lax.dynamic_slice_in_dim(down_weight, other_index * half_width, half_width, 1)
    other_down = lax.ppermute(their_down, "mp", mp_route)
    seg_packed = jnp.concatenate([seg_peak[..., None], seg_total[..., None], seg_acc], axis=-1)
    seg_packed, other_up, other_down = lax.optimization_barrier((seg_packed, other_up, other_down))
    merged = tree_merge(seg_packed, "seq")
    global_out = merged[..., 2:] / merged[..., 1:2]
    attn_rows = sparse_out.reshape(tok_rows, local_width)
    for which in range(GLOB):
        global_id = global_blocks[which]
        start_row = global_id % QB_DEV * BLK
        current = lax.dynamic_slice_in_dim(attn_rows, start_row, BLK, 0)
        replacing = global_out[which].transpose(1, 0, 2).reshape(BLK, local_width)
        is_owner = global_id // QB_DEV == my_shard
        attn_rows = lax.dynamic_update_slice_in_dim(
            attn_rows, jnp.where(is_owner, replacing, current), start_row, 0
        )
    attention = attn_rows.astype(jnp.bfloat16)
    other_attention = lax.ppermute(attention, "mp", mp_route)
    other_weight = lax.ppermute(out_weight, "mp", mp_route)
    projected = jnp.dot(attention, out_weight, preferred_element_type=jnp.float32) + jnp.dot(
        other_attention, other_weight, preferred_element_type=jnp.float32
    )
    middle = (residual_in.astype(jnp.float32) + projected).astype(jnp.bfloat16)
    middle_own = lax.dynamic_slice_in_dim(middle, mp_index * half_width, half_width, 1)
    middle32 = middle.astype(jnp.float32)
    row_mean = jnp.mean(middle32, axis=1, keepdims=True)
    centered = middle32 - row_mean
    row_var = jnp.mean(centered * centered, axis=1, keepdims=True)
    normed = (centered * lax.rsqrt(row_var + 1e-05) * norm_gain).astype(jnp.bfloat16)
    own_down = lax.dynamic_slice_in_dim(down_weight, mp_index * half_width, half_width, 1)
    hidden_own = jax.nn.gelu(
        jnp.dot(normed, up_weight, preferred_element_type=jnp.float32), approximate=True
    ).astype(jnp.bfloat16)
    hidden_other = jax.nn.gelu(
        jnp.dot(normed, other_up, preferred_element_type=jnp.float32), approximate=True
    ).astype(jnp.bfloat16)
    down_part = jnp.dot(hidden_own, own_down, preferred_element_type=jnp.float32) + jnp.dot(
        hidden_other, other_down, preferred_element_type=jnp.float32
    )
    return (middle_own.astype(jnp.float32) + down_part).astype(jnp.bfloat16)


def solution(mesh):
    placed = (
        P("seq", None),
        P("seq", "mp"),
        P("seq", "mp"),
        P("seq", "mp"),
        P(None, "mp", None),
        P(),
        P("mp", None),
        P(),
        P(None, "mp"),
        P("mp", None),
    )
    return jax.shard_map(
        local, mesh=mesh, in_specs=placed, out_specs=P("seq", "mp"), check_vma=False
    )
```

```python
import math

import jax
import jax.numpy as jnp
from jax import lax
from jax.sharding import PartitionSpec as P

HD = 64
BLK = 64
R = 3
GLOB = 2
GROUP = 16
QB_DEV = 16


def with_halo(block, sides, width):
    for axis, dim in sides:
        count = lax.axis_size(axis)
        forward = [(i, i + 1) for i in range(count - 1)]
        backward = [(target, source) for source, target in forward]
        low = lax.ppermute(
            lax.slice_in_dim(block, block.shape[dim] - width, None, axis=dim), axis, forward
        )
        high = lax.ppermute(lax.slice_in_dim(block, 0, width, axis=dim), axis, backward)
        block = jnp.concatenate([low, block, high], axis=dim)
    return block


def swapped(block, axis, apart):
    count = lax.axis_size(axis)
    route = []
    for low in range(count):
        high = low | 1 << apart
        if high != low and high < count:
            route += [(low, high), (high, low)]
    return lax.ppermute(block, axis, route)


def xor_partners(block, axis, low_bit, width):
    count = lax.axis_size(axis)
    return [
        lax.ppermute(block, axis, [(i, i ^ k << low_bit) for i in range(count)])
        for k in range(1, 1 << width)
    ]


def tree_stages(axis):
    bits = lax.axis_size(axis).bit_length() - 1
    return [(low, min(2, bits - low)) for low in range(0, bits, 2)]


def tree_sum(block, axis):
    for low_bit, width in tree_stages(axis):
        for part in xor_partners(block, axis, low_bit, width):
            block = block + part
    return block


def merge_packed(parts):
    larger = parts[0][..., :1]
    for part in parts[1:]:
        larger = jnp.maximum(larger, part[..., :1])
    mixed = parts[0][..., 1:] * jnp.exp(parts[0][..., :1] - larger)
    for part in parts[1:]:
        mixed = mixed + part[..., 1:] * jnp.exp(part[..., :1] - larger)
    return jnp.concatenate([larger, mixed], axis=-1)


def tree_merge(packed, axis):
    for low_bit, width in tree_stages(axis):
        packed = merge_packed([packed] + xor_partners(packed, axis, low_bit, width))
    return packed


def local(
    residual_in,
    query_rows,
    key_rows,
    value_rows,
    rand_blocks,
    global_blocks,
    out_weight,
    norm_gain,
    up_weight,
    down_weight,
):
    tok_rows = query_rows.shape[0]
    local_width = query_rows.shape[1]
    heads_here = local_width // HD
    shard_count = lax.axis_size("seq")
    my_shard = lax.axis_index("seq")
    total_blocks = QB_DEV * shard_count
    score_scale = 1.0 / math.sqrt(HD)
    q_heads = query_rows.reshape(QB_DEV, BLK, heads_here, HD)
    key_heads = key_rows.reshape(tok_rows, heads_here, HD)
    value_heads = value_rows.reshape(tok_rows, heads_here, HD)
    kv_tokens = jnp.concatenate([key_heads, value_heads], axis=2)
    padded = with_halo(kv_tokens, (("seq", 0),), BLK)
    padded_blocks = padded.reshape(QB_DEV + 2, BLK, heads_here, 2 * HD).transpose(0, 2, 1, 3)
    own_blocks = padded_blocks[1:-1]
    window_kv = jnp.stack([padded_blocks[:-2], own_blocks, padded_blocks[2:]], axis=2)
    flat_kv = own_blocks.reshape(QB_DEV * heads_here, BLK, 2 * HD)
    position = my_shard % GROUP
    group_base = my_shard - position
    slot_count = QB_DEV * heads_here * R
    capacity = slot_count // GROUP
    offsets_all = jnp.arange(GROUP, dtype=jnp.int32)
    slot_heads = jnp.arange(slot_count, dtype=jnp.int32) // R % heads_here
    cap_range = jnp.arange(capacity, dtype=jnp.int32)

    def requests_of(shard):
        request_rows = lax.dynamic_slice_in_dim(rand_blocks, shard * QB_DEV, QB_DEV, 0)
        return request_rows.reshape(slot_count)

    def payload_for(offset):
        requester = group_base + (position - offset) % GROUP
        wanted = requests_of(requester)
        from_me = wanted // QB_DEV == my_shard
        order_rank = jnp.cumsum(from_me.astype(jnp.int32)) - 1
        source = wanted % QB_DEV * heads_here + slot_heads
        pick_table = from_me[:, None] & (order_rank[:, None] == cap_range[None, :])
        chosen = jnp.sum(jnp.where(pick_table, source[:, None], 0), axis=0)
        return jnp.take(flat_kv, chosen, axis=0)

    my_requests = requests_of(my_shard)
    owner_offset = (my_requests // QB_DEV - group_base - position) % GROUP
    offset_hits = owner_offset[:, None] == offsets_all[None, :]
    rank_table = jnp.cumsum(offset_hits.astype(jnp.int32), axis=0) - 1
    my_rank = jnp.sum(jnp.where(offset_hits, rank_table, 0), axis=1)
    slot_index = owner_offset * capacity + my_rank
    sectioned = jax.vmap(payload_for)(offsets_all)
    packed = jnp.stack([query_rows, key_rows, value_rows], axis=0)
    contributions = []
    for which in range(GLOB):
        global_id = global_blocks[which]
        block_rows = lax.dynamic_slice_in_dim(packed, global_id % QB_DEV * BLK, BLK, 1)
        is_owner = global_id // QB_DEV == my_shard
        contributions.append(jnp.where(is_owner, block_rows, jnp.zeros_like(block_rows)))

    global_packed = tree_sum(jnp.stack(contributions, axis=0), "seq")
    sectioned, global_packed = lax.optimization_barrier((sectioned, global_packed))
    shard_ids = range(shard_count)
    arrived = [sectioned[0]]
    for offset in range(1, GROUP):
        route = [(s, s - s % GROUP + (s % GROUP - offset) % GROUP) for s in shard_ids]
        arrived.append(lax.ppermute(sectioned[offset], "seq", route))
    received = jnp.stack(arrived, axis=0)
    random_kv = jnp.take(received.reshape(GROUP * capacity, BLK, 2 * HD), slot_index, axis=0)
    random_kv = random_kv.reshape(QB_DEV, heads_here, R, BLK, 2 * HD)
    global_q = global_packed[:, 0].reshape(GLOB, BLK, heads_here, HD)
    global_k = global_packed[:, 1].reshape(GLOB, BLK, heads_here, HD)
    global_v = global_packed[:, 2].reshape(GLOB, BLK, heads_here, HD)
    global_kv = jnp.concatenate([global_k, global_v], axis=3).transpose(2, 0, 1, 3)
    global_kv = jnp.broadcast_to(global_kv[None], (QB_DEV, heads_here, GLOB, BLK, 2 * HD))
    all_kv = jnp.concatenate([window_kv, random_kv, global_kv], axis=2)
    keys_all = all_kv[..., :HD]
    values_all = all_kv[..., HD:]
    scores = (
        jnp.einsum("bqhd,bhjkd->bhqjk", q_heads, keys_all, preferred_element_type=jnp.float32)
        * score_scale
    )
    block_global = my_shard * QB_DEV + jnp.arange(QB_DEV, dtype=jnp.int32)
    valid_cols = jnp.concatenate(
        [
            (block_global >= 1)[:, None],
            jnp.ones((QB_DEV, 1), dtype=bool),
            (block_global + 1 < total_blocks)[:, None],
            jnp.ones((QB_DEV, R + GLOB), dtype=bool),
        ],
        axis=1,
    )
    scores = jnp.where(valid_cols[:, None, None, :, None], scores, jnp.float32(-1e30))
    row_peak = jnp.max(scores, axis=(3, 4), keepdims=True)
    weights = jnp.exp(scores - row_peak)
    row_total = jnp.sum(weights, axis=(3, 4))
    mixed_sum = jnp.einsum(
        "bhqjk,bhjkd->bqhd",
        weights.astype(jnp.bfloat16),
        values_all,
        preferred_element_type=jnp.float32,
    )
    sparse_out = mixed_sum / row_total.transpose(0, 2, 1)[..., None]
    global_scores = (
        jnp.einsum("gqhd,thd->ghqt", global_q, key_heads, preferred_element_type=jnp.float32)
        * score_scale
    )
    seg_peak = jnp.max(global_scores, axis=3)
    seg_weights = jnp.exp(global_scores - seg_peak[..., None])
    seg_total = jnp.sum(seg_weights, axis=3)
    seg_acc = jnp.einsum(
        "ghqt,thd->ghqd",
        seg_weights.astype(jnp.bfloat16),
        value_heads,
        preferred_element_type=jnp.float32,
    )
    mp_index = lax.axis_index("mp")
    mp_route = [(0, 1), (1, 0)]
    half_width = residual_in.shape[1] // lax.axis_size("mp")
    other_index = 1 - mp_index
    their_down = lax.dynamic_slice_in_dim(down_weight, other_index * half_width, half_width, 1)
    _, late_up, late_down, late_out = lax.optimization_barrier(
        (global_packed, up_weight, their_down, out_weight)
    )
    other_up = lax.ppermute(late_up, "mp", mp_route)
    other_down = lax.ppermute(late_down, "mp", mp_route)
    seg_packed = jnp.concatenate([seg_peak[..., None], seg_total[..., None], seg_acc], axis=-1)
    seg_packed, other_up, other_down = lax.optimization_barrier((seg_packed, other_up, other_down))
    merged = tree_merge(seg_packed, "seq")
    global_out = merged[..., 2:] / merged[..., 1:2]
    attn_rows = sparse_out.reshape(tok_rows, local_width)
    for which in range(GLOB):
        global_id = global_blocks[which]
        start_row = global_id % QB_DEV * BLK
        current = lax.dynamic_slice_in_dim(attn_rows, start_row, BLK, 0)
        replacing = global_out[which].transpose(1, 0, 2).reshape(BLK, local_width)
        is_owner = global_id // QB_DEV == my_shard
        attn_rows = lax.dynamic_update_slice_in_dim(
            attn_rows, jnp.where(is_owner, replacing, current), start_row, 0
        )
    attention = attn_rows.astype(jnp.bfloat16)
    other_attention = lax.ppermute(attention, "mp", mp_route)
    other_weight = lax.ppermute(late_out, "mp", mp_route)
    projected = jnp.dot(attention, out_weight, preferred_element_type=jnp.float32) + jnp.dot(
        other_attention, other_weight, preferred_element_type=jnp.float32
    )
    middle = (residual_in.astype(jnp.float32) + projected).astype(jnp.bfloat16)
    middle_own = lax.dynamic_slice_in_dim(middle, mp_index * half_width, half_width, 1)
    middle32 = middle.astype(jnp.float32)
    row_mean = jnp.mean(middle32, axis=1, keepdims=True)
    centered = middle32 - row_mean
    row_var = jnp.mean(centered * centered, axis=1, keepdims=True)
    normed = (centered * lax.rsqrt(row_var + 1e-05) * norm_gain).astype(jnp.bfloat16)
    own_down = lax.dynamic_slice_in_dim(down_weight, mp_index * half_width, half_width, 1)
    hidden_own = jax.nn.gelu(
        jnp.dot(normed, up_weight, preferred_element_type=jnp.float32), approximate=True
    ).astype(jnp.bfloat16)
    hidden_other = jax.nn.gelu(
        jnp.dot(normed, other_up, preferred_element_type=jnp.float32), approximate=True
    ).astype(jnp.bfloat16)
    down_part = jnp.dot(hidden_own, own_down, preferred_element_type=jnp.float32) + jnp.dot(
        hidden_other, other_down, preferred_element_type=jnp.float32
    )
    return (middle_own.astype(jnp.float32) + down_part).astype(jnp.bfloat16)


def solution(mesh):
    placed = (
        P("seq", None),
        P("seq", "mp"),
        P("seq", "mp"),
        P("seq", "mp"),
        P(None, "mp", None),
        P(),
        P("mp", None),
        P(),
        P(None, "mp"),
        P("mp", None),
    )
    return jax.shard_map(
        local, mesh=mesh, in_specs=placed, out_specs=P("seq", "mp"), check_vma=False
    )
```

```python
import math

import jax
import jax.numpy as jnp
from jax import lax
from jax.sharding import PartitionSpec as P

HD = 64
BLK = 64
R = 3
GLOB = 2
GROUP = 16
QB_DEV = 16


def with_halo(block, sides, width):
    for axis, dim in sides:
        count = lax.axis_size(axis)
        forward = [(i, i + 1) for i in range(count - 1)]
        backward = [(target, source) for source, target in forward]
        low = lax.ppermute(
            lax.slice_in_dim(block, block.shape[dim] - width, None, axis=dim), axis, forward
        )
        high = lax.ppermute(lax.slice_in_dim(block, 0, width, axis=dim), axis, backward)
        block = jnp.concatenate([low, block, high], axis=dim)
    return block


def swapped(block, axis, apart):
    count = lax.axis_size(axis)
    route = []
    for low in range(count):
        high = low | 1 << apart
        if high != low and high < count:
            route += [(low, high), (high, low)]
    return lax.ppermute(block, axis, route)


def xor_partners(block, axis, low_bit, width):
    count = lax.axis_size(axis)
    return [
        lax.ppermute(block, axis, [(i, i ^ k << low_bit) for i in range(count)])
        for k in range(1, 1 << width)
    ]


def tree_stages(axis):
    bits = lax.axis_size(axis).bit_length() - 1
    return [(low, min(2, bits - low)) for low in range(0, bits, 2)]


def tree_sum(block, axis):
    for low_bit, width in tree_stages(axis):
        for part in xor_partners(block, axis, low_bit, width):
            block = block + part
    return block


def merge_packed(parts):
    larger = parts[0][..., :1]
    for part in parts[1:]:
        larger = jnp.maximum(larger, part[..., :1])
    mixed = parts[0][..., 1:] * jnp.exp(parts[0][..., :1] - larger)
    for part in parts[1:]:
        mixed = mixed + part[..., 1:] * jnp.exp(part[..., :1] - larger)
    return jnp.concatenate([larger, mixed], axis=-1)


def tree_merge(packed, axis):
    for low_bit, width in tree_stages(axis):
        packed = merge_packed([packed] + xor_partners(packed, axis, low_bit, width))
    return packed


def local(
    residual_in,
    query_rows,
    key_rows,
    value_rows,
    rand_blocks,
    global_blocks,
    out_weight,
    norm_gain,
    up_weight,
    down_weight,
):
    tok_rows = query_rows.shape[0]
    local_width = query_rows.shape[1]
    heads_here = local_width // HD
    shard_count = lax.axis_size("seq")
    my_shard = lax.axis_index("seq")
    total_blocks = QB_DEV * shard_count
    score_scale = 1.0 / math.sqrt(HD)
    q_heads = query_rows.reshape(QB_DEV, BLK, heads_here, HD)
    key_heads = key_rows.reshape(tok_rows, heads_here, HD)
    value_heads = value_rows.reshape(tok_rows, heads_here, HD)
    kv_tokens = jnp.concatenate([key_heads, value_heads], axis=2)
    padded = with_halo(kv_tokens, (("seq", 0),), BLK)
    padded_blocks = padded.reshape(QB_DEV + 2, BLK, heads_here, 2 * HD).transpose(0, 2, 1, 3)
    own_blocks = padded_blocks[1:-1]
    window_kv = jnp.stack([padded_blocks[:-2], own_blocks, padded_blocks[2:]], axis=2)
    flat_kv = (
        kv_tokens.reshape(QB_DEV, BLK, heads_here, 2 * HD)
        .transpose(0, 2, 1, 3)
        .reshape(QB_DEV * heads_here, BLK, 2 * HD)
    )
    position = my_shard % GROUP
    group_base = my_shard - position
    slot_count = QB_DEV * heads_here * R
    capacity = slot_count // GROUP
    offsets_all = jnp.arange(GROUP, dtype=jnp.int32)
    slot_heads = jnp.arange(slot_count, dtype=jnp.int32) // R % heads_here
    cap_range = jnp.arange(capacity, dtype=jnp.int32)

    def requests_of(shard):
        request_rows = lax.dynamic_slice_in_dim(rand_blocks, shard * QB_DEV, QB_DEV, 0)
        return request_rows.reshape(slot_count)

    def payload_for(offset):
        requester = group_base + (position - offset) % GROUP
        wanted = requests_of(requester)
        from_me = wanted // QB_DEV == my_shard
        order_rank = jnp.cumsum(from_me.astype(jnp.int32)) - 1
        source = wanted % QB_DEV * heads_here + slot_heads
        pick_table = from_me[:, None] & (order_rank[:, None] == cap_range[None, :])
        chosen = jnp.sum(jnp.where(pick_table, source[:, None], 0), axis=0)
        return jnp.take(flat_kv, chosen, axis=0)

    my_requests = requests_of(my_shard)
    owner_offset = (my_requests // QB_DEV - group_base - position) % GROUP
    offset_hits = owner_offset[:, None] == offsets_all[None, :]
    rank_table = jnp.cumsum(offset_hits.astype(jnp.int32), axis=0) - 1
    my_rank = jnp.sum(jnp.where(offset_hits, rank_table, 0), axis=1)
    slot_index = owner_offset * capacity + my_rank
    sectioned = jax.vmap(payload_for)(offsets_all)
    shard_ids = range(shard_count)
    arrived = [sectioned[0]]
    for offset in range(1, GROUP):
        route = [(s, s - s % GROUP + (s % GROUP - offset) % GROUP) for s in shard_ids]
        arrived.append(lax.ppermute(sectioned[offset], "seq", route))
    received = jnp.stack(arrived, axis=0)
    random_kv = jnp.take(received.reshape(GROUP * capacity, BLK, 2 * HD), slot_index, axis=0)
    random_kv = random_kv.reshape(QB_DEV, heads_here, R, BLK, 2 * HD)
    packed = jnp.stack([query_rows, key_rows, value_rows], axis=0)
    contributions = []
    for which in range(GLOB):
        global_id = global_blocks[which]
        block_rows = lax.dynamic_slice_in_dim(packed, global_id % QB_DEV * BLK, BLK, 1)
        is_owner = global_id // QB_DEV == my_shard
        contributions.append(jnp.where(is_owner, block_rows, jnp.zeros_like(block_rows)))
    global_packed = tree_sum(jnp.stack(contributions, axis=0), "seq")
    global_q = global_packed[:, 0].reshape(GLOB, BLK, heads_here, HD)
    global_k = global_packed[:, 1].reshape(GLOB, BLK, heads_here, HD)
    global_v = global_packed[:, 2].reshape(GLOB, BLK, heads_here, HD)
    global_kv = jnp.concatenate([global_k, global_v], axis=3).transpose(2, 0, 1, 3)
    global_kv = jnp.broadcast_to(global_kv[None], (QB_DEV, heads_here, GLOB, BLK, 2 * HD))
    all_kv = jnp.concatenate([window_kv, random_kv, global_kv], axis=2)
    keys_all = all_kv[..., :HD]
    values_all = all_kv[..., HD:]
    scores = (
        jnp.einsum("bqhd,bhjkd->bhqjk", q_heads, keys_all, preferred_element_type=jnp.float32)
        * score_scale
    )
    block_global = my_shard * QB_DEV + jnp.arange(QB_DEV, dtype=jnp.int32)
    valid_cols = jnp.concatenate(
        [
            (block_global >= 1)[:, None],
            jnp.ones((QB_DEV, 1), dtype=bool),
            (block_global + 1 < total_blocks)[:, None],
            jnp.ones((QB_DEV, R + GLOB), dtype=bool),
        ],
        axis=1,
    )
    scores = jnp.where(valid_cols[:, None, None, :, None], scores, jnp.float32(-1e30))
    row_peak = jnp.max(scores, axis=(3, 4), keepdims=True)
    weights = jnp.exp(scores - row_peak)
    row_total = jnp.sum(weights, axis=(3, 4))
    mixed_sum = jnp.einsum(
        "bhqjk,bhjkd->bqhd",
        weights.astype(jnp.bfloat16),
        values_all,
        preferred_element_type=jnp.float32,
    )
    sparse_out = mixed_sum / row_total.transpose(0, 2, 1)[..., None]
    global_scores = (
        jnp.einsum("gqhd,thd->ghqt", global_q, key_heads, preferred_element_type=jnp.float32)
        * score_scale
    )
    seg_peak = jnp.max(global_scores, axis=3)
    seg_weights = jnp.exp(global_scores - seg_peak[..., None])
    seg_total = jnp.sum(seg_weights, axis=3)
    seg_acc = jnp.einsum(
        "ghqt,thd->ghqd",
        seg_weights.astype(jnp.bfloat16),
        value_heads,
        preferred_element_type=jnp.float32,
    )
    mp_index = lax.axis_index("mp")
    mp_route = [(0, 1), (1, 0)]
    half_width = residual_in.shape[1] // lax.axis_size("mp")
    other_up = lax.ppermute(up_weight, "mp", mp_route)
    other_index = 1 - mp_index
    their_down = lax.dynamic_slice_in_dim(down_weight, other_index * half_width, half_width, 1)
    other_down = lax.ppermute(their_down, "mp", mp_route)
    seg_packed = jnp.concatenate([seg_peak[..., None], seg_total[..., None], seg_acc], axis=-1)
    seg_packed, other_up, other_down = lax.optimization_barrier((seg_packed, other_up, other_down))
    merged = tree_merge(seg_packed, "seq")
    global_out = merged[..., 2:] / merged[..., 1:2]
    attn_rows = sparse_out.reshape(tok_rows, local_width)
    for which in range(GLOB):
        global_id = global_blocks[which]
        start_row = global_id % QB_DEV * BLK
        current = lax.dynamic_slice_in_dim(attn_rows, start_row, BLK, 0)
        replacing = global_out[which].transpose(1, 0, 2).reshape(BLK, local_width)
        is_owner = global_id // QB_DEV == my_shard
        attn_rows = lax.dynamic_update_slice_in_dim(
            attn_rows, jnp.where(is_owner, replacing, current), start_row, 0
        )
    attention = attn_rows.astype(jnp.bfloat16)
    other_attention = lax.ppermute(attention, "mp", mp_route)
    other_weight = lax.ppermute(out_weight, "mp", mp_route)
    projected = jnp.dot(attention, out_weight, preferred_element_type=jnp.float32) + jnp.dot(
        other_attention, other_weight, preferred_element_type=jnp.float32
    )
    middle = (residual_in.astype(jnp.float32) + projected).astype(jnp.bfloat16)
    middle_own = lax.dynamic_slice_in_dim(middle, mp_index * half_width, half_width, 1)
    middle32 = middle.astype(jnp.float32)
    row_mean = jnp.mean(middle32, axis=1, keepdims=True)
    centered = middle32 - row_mean
    row_var = jnp.mean(centered * centered, axis=1, keepdims=True)
    normed = (centered * lax.rsqrt(row_var + 1e-05) * norm_gain).astype(jnp.bfloat16)
    own_down = lax.dynamic_slice_in_dim(down_weight, mp_index * half_width, half_width, 1)
    hidden_own = jax.nn.gelu(
        jnp.dot(normed, up_weight, preferred_element_type=jnp.float32), approximate=True
    ).astype(jnp.bfloat16)
    hidden_other = jax.nn.gelu(
        jnp.dot(normed, other_up, preferred_element_type=jnp.float32), approximate=True
    ).astype(jnp.bfloat16)
    down_part = jnp.dot(hidden_own, own_down, preferred_element_type=jnp.float32) + jnp.dot(
        hidden_other, other_down, preferred_element_type=jnp.float32
    )
    return (middle_own.astype(jnp.float32) + down_part).astype(jnp.bfloat16)


def solution(mesh):
    placed = (
        P("seq", None),
        P("seq", "mp"),
        P("seq", "mp"),
        P("seq", "mp"),
        P(None, "mp", None),
        P(),
        P("mp", None),
        P(),
        P(None, "mp"),
        P("mp", None),
    )
    return jax.shard_map(
        local, mesh=mesh, in_specs=placed, out_specs=P("seq", "mp"), check_vma=False
    )
```

```python
import math

import jax
import jax.numpy as jnp
from jax import lax
from jax.sharding import PartitionSpec as P

HD = 64
BLK = 64
R = 3
GLOB = 2
GROUP = 16
QB_DEV = 16


def with_halo(block, sides, width):
    for axis, dim in sides:
        count = lax.axis_size(axis)
        forward = [(i, i + 1) for i in range(count - 1)]
        backward = [(target, source) for source, target in forward]
        low = lax.ppermute(
            lax.slice_in_dim(block, block.shape[dim] - width, None, axis=dim), axis, forward
        )
        high = lax.ppermute(lax.slice_in_dim(block, 0, width, axis=dim), axis, backward)
        block = jnp.concatenate([low, block, high], axis=dim)
    return block


def swapped(block, axis, apart):
    count = lax.axis_size(axis)
    route = []
    for low in range(count):
        high = low | 1 << apart
        if high != low and high < count:
            route += [(low, high), (high, low)]
    return lax.ppermute(block, axis, route)


def xor_partners(block, axis, low_bit, width):
    count = lax.axis_size(axis)
    return [
        lax.ppermute(block, axis, [(i, i ^ k << low_bit) for i in range(count)])
        for k in range(1, 1 << width)
    ]


def tree_stages(axis):
    bits = lax.axis_size(axis).bit_length() - 1
    return [(low, min(2, bits - low)) for low in range(0, bits, 2)]


def tree_sum(block, axis):
    stages = []
    for low_bit, width in reversed(tree_stages(axis)):
        for part in xor_partners(block, axis, low_bit, width):
            block = block + part
        stages.append(block)
    return block, stages[0]


def merge_packed(parts):
    larger = parts[0][..., :1]
    for part in parts[1:]:
        larger = jnp.maximum(larger, part[..., :1])
    mixed = parts[0][..., 1:] * jnp.exp(parts[0][..., :1] - larger)
    for part in parts[1:]:
        mixed = mixed + part[..., 1:] * jnp.exp(part[..., :1] - larger)
    return jnp.concatenate([larger, mixed], axis=-1)


def tree_merge(packed, axis):
    for low_bit, width in tree_stages(axis):
        packed = merge_packed([packed] + xor_partners(packed, axis, low_bit, width))
    return packed


def local(
    residual_in,
    query_rows,
    key_rows,
    value_rows,
    rand_blocks,
    global_blocks,
    out_weight,
    norm_gain,
    up_weight,
    down_weight,
):
    tok_rows = query_rows.shape[0]
    local_width = query_rows.shape[1]
    heads_here = local_width // HD
    shard_count = lax.axis_size("seq")
    my_shard = lax.axis_index("seq")
    total_blocks = QB_DEV * shard_count
    score_scale = 1.0 / math.sqrt(HD)
    q_heads = query_rows.reshape(QB_DEV, BLK, heads_here, HD)
    key_heads = key_rows.reshape(tok_rows, heads_here, HD)
    value_heads = value_rows.reshape(tok_rows, heads_here, HD)
    kv_tokens = jnp.concatenate([key_heads, value_heads], axis=2)
    padded = with_halo(kv_tokens, (("seq", 0),), BLK)
    padded_blocks = padded.reshape(QB_DEV + 2, BLK, heads_here, 2 * HD).transpose(0, 2, 1, 3)
    own_blocks = padded_blocks[1:-1]
    window_kv = jnp.stack([padded_blocks[:-2], own_blocks, padded_blocks[2:]], axis=2)
    flat_kv = (
        kv_tokens.reshape(QB_DEV, BLK, heads_here, 2 * HD)
        .transpose(0, 2, 1, 3)
        .reshape(QB_DEV * heads_here, BLK, 2 * HD)
    )
    position = my_shard % GROUP
    group_base = my_shard - position
    slot_count = QB_DEV * heads_here * R
    capacity = slot_count // GROUP
    offsets_all = jnp.arange(GROUP, dtype=jnp.int32)
    slot_heads = jnp.arange(slot_count, dtype=jnp.int32) // R % heads_here
    cap_range = jnp.arange(capacity, dtype=jnp.int32)

    def requests_of(shard):
        request_rows = lax.dynamic_slice_in_dim(rand_blocks, shard * QB_DEV, QB_DEV, 0)
        return request_rows.reshape(slot_count)

    def payload_for(offset):
        requester = group_base + (position - offset) % GROUP
        wanted = requests_of(requester)
        from_me = wanted // QB_DEV == my_shard
        order_rank = jnp.cumsum(from_me.astype(jnp.int32)) - 1
        source = wanted % QB_DEV * heads_here + slot_heads
        pick_table = from_me[:, None] & (order_rank[:, None] == cap_range[None, :])
        chosen = jnp.sum(jnp.where(pick_table, source[:, None], 0), axis=0)
        return jnp.take(flat_kv, chosen, axis=0)

    my_requests = requests_of(my_shard)
    owner_offset = (my_requests // QB_DEV - group_base - position) % GROUP
    offset_hits = owner_offset[:, None] == offsets_all[None, :]
    rank_table = jnp.cumsum(offset_hits.astype(jnp.int32), axis=0) - 1
    my_rank = jnp.sum(jnp.where(offset_hits, rank_table, 0), axis=1)
    slot_index = owner_offset * capacity + my_rank
    sectioned = jax.vmap(payload_for)(offsets_all)
    shard_ids = range(shard_count)
    arrived = [sectioned[0]]
    for offset in range(1, GROUP):
        route = [(s, s - s % GROUP + (s % GROUP - offset) % GROUP) for s in shard_ids]
        arrived.append(lax.ppermute(sectioned[offset], "seq", route))
    received = jnp.stack(arrived, axis=0)
    random_kv = jnp.take(received.reshape(GROUP * capacity, BLK, 2 * HD), slot_index, axis=0)
    random_kv = random_kv.reshape(QB_DEV, heads_here, R, BLK, 2 * HD)
    packed = jnp.stack([query_rows, key_rows, value_rows], axis=0)
    contributions = []
    for which in range(GLOB):
        global_id = global_blocks[which]
        block_rows = lax.dynamic_slice_in_dim(packed, global_id % QB_DEV * BLK, BLK, 1)
        is_owner = global_id // QB_DEV == my_shard
        contributions.append(jnp.where(is_owner, block_rows, jnp.zeros_like(block_rows)))
    global_packed, first_stage = tree_sum(jnp.stack(contributions, axis=0), "seq")
    mp_index = lax.axis_index("mp")
    mp_route = [(0, 1), (1, 0)]
    half_width = residual_in.shape[1] // lax.axis_size("mp")
    other_index = 1 - mp_index
    their_down = lax.dynamic_slice_in_dim(down_weight, other_index * half_width, half_width, 1)
    _, late_up, late_down, late_out = lax.optimization_barrier(
        (first_stage, up_weight, their_down, out_weight)
    )
    other_up = lax.ppermute(late_up, "mp", mp_route)
    other_down = lax.ppermute(late_down, "mp", mp_route)
    other_weight = lax.ppermute(late_out, "mp", mp_route)
    global_q = global_packed[:, 0].reshape(GLOB, BLK, heads_here, HD)
    global_k = global_packed[:, 1].reshape(GLOB, BLK, heads_here, HD)
    global_v = global_packed[:, 2].reshape(GLOB, BLK, heads_here, HD)
    global_kv = jnp.concatenate([global_k, global_v], axis=3).transpose(2, 0, 1, 3)
    global_kv = jnp.broadcast_to(global_kv[None], (QB_DEV, heads_here, GLOB, BLK, 2 * HD))
    all_kv = jnp.concatenate([window_kv, random_kv, global_kv], axis=2)
    keys_all = all_kv[..., :HD]
    values_all = all_kv[..., HD:]
    scores = (
        jnp.einsum("bqhd,bhjkd->bhqjk", q_heads, keys_all, preferred_element_type=jnp.float32)
        * score_scale
    )
    block_global = my_shard * QB_DEV + jnp.arange(QB_DEV, dtype=jnp.int32)
    valid_cols = jnp.concatenate(
        [
            (block_global >= 1)[:, None],
            jnp.ones((QB_DEV, 1), dtype=bool),
            (block_global + 1 < total_blocks)[:, None],
            jnp.ones((QB_DEV, R + GLOB), dtype=bool),
        ],
        axis=1,
    )
    scores = jnp.where(valid_cols[:, None, None, :, None], scores, jnp.float32(-1e30))
    row_peak = jnp.max(scores, axis=(3, 4), keepdims=True)
    weights = jnp.exp(scores - row_peak)
    row_total = jnp.sum(weights, axis=(3, 4))
    mixed_sum = jnp.einsum(
        "bhqjk,bhjkd->bqhd",
        weights.astype(jnp.bfloat16),
        values_all,
        preferred_element_type=jnp.float32,
    )
    sparse_out = mixed_sum / row_total.transpose(0, 2, 1)[..., None]
    global_scores = (
        jnp.einsum("gqhd,thd->ghqt", global_q, key_heads, preferred_element_type=jnp.float32)
        * score_scale
    )
    seg_peak = jnp.max(global_scores, axis=3)
    seg_weights = jnp.exp(global_scores - seg_peak[..., None])
    seg_total = jnp.sum(seg_weights, axis=3)
    seg_acc = jnp.einsum(
        "ghqt,thd->ghqd",
        seg_weights.astype(jnp.bfloat16),
        value_heads,
        preferred_element_type=jnp.float32,
    )
    seg_packed = jnp.concatenate([seg_peak[..., None], seg_total[..., None], seg_acc], axis=-1)
    seg_packed, other_up, other_down = lax.optimization_barrier((seg_packed, other_up, other_down))
    merged = tree_merge(seg_packed, "seq")
    global_out = merged[..., 2:] / merged[..., 1:2]
    attn_rows = sparse_out.reshape(tok_rows, local_width)
    for which in range(GLOB):
        global_id = global_blocks[which]
        start_row = global_id % QB_DEV * BLK
        current = lax.dynamic_slice_in_dim(attn_rows, start_row, BLK, 0)
        replacing = global_out[which].transpose(1, 0, 2).reshape(BLK, local_width)
        is_owner = global_id // QB_DEV == my_shard
        attn_rows = lax.dynamic_update_slice_in_dim(
            attn_rows, jnp.where(is_owner, replacing, current), start_row, 0
        )
    attention = attn_rows.astype(jnp.bfloat16)
    other_attention = lax.ppermute(attention, "mp", mp_route)
    projected = jnp.dot(attention, out_weight, preferred_element_type=jnp.float32) + jnp.dot(
        other_attention, other_weight, preferred_element_type=jnp.float32
    )
    middle = (residual_in.astype(jnp.float32) + projected).astype(jnp.bfloat16)
    middle_own = lax.dynamic_slice_in_dim(middle, mp_index * half_width, half_width, 1)
    middle32 = middle.astype(jnp.float32)
    row_mean = jnp.mean(middle32, axis=1, keepdims=True)
    centered = middle32 - row_mean
    row_var = jnp.mean(centered * centered, axis=1, keepdims=True)
    normed = (centered * lax.rsqrt(row_var + 1e-05) * norm_gain).astype(jnp.bfloat16)
    own_down = lax.dynamic_slice_in_dim(down_weight, mp_index * half_width, half_width, 1)
    hidden_own = jax.nn.gelu(
        jnp.dot(normed, up_weight, preferred_element_type=jnp.float32), approximate=True
    ).astype(jnp.bfloat16)
    hidden_other = jax.nn.gelu(
        jnp.dot(normed, other_up, preferred_element_type=jnp.float32), approximate=True
    ).astype(jnp.bfloat16)
    down_part = jnp.dot(hidden_own, own_down, preferred_element_type=jnp.float32) + jnp.dot(
        hidden_other, other_down, preferred_element_type=jnp.float32
    )
    return (middle_own.astype(jnp.float32) + down_part).astype(jnp.bfloat16)


def solution(mesh):
    placed = (
        P("seq", None),
        P("seq", "mp"),
        P("seq", "mp"),
        P("seq", "mp"),
        P(None, "mp", None),
        P(),
        P("mp", None),
        P(),
        P(None, "mp"),
        P("mp", None),
    )
    return jax.shard_map(
        local, mesh=mesh, in_specs=placed, out_specs=P("seq", "mp"), check_vma=False
    )
```

```python
import math

import jax
import jax.numpy as jnp
from jax import lax
from jax.sharding import PartitionSpec as P

HD = 64
BLK = 64
R = 3
GLOB = 2
GROUP = 16
QB_DEV = 16


def with_halo(block, sides, width):
    for axis, dim in sides:
        count = lax.axis_size(axis)
        forward = [(i, i + 1) for i in range(count - 1)]
        backward = [(target, source) for source, target in forward]
        low = lax.ppermute(
            lax.slice_in_dim(block, block.shape[dim] - width, None, axis=dim), axis, forward
        )
        high = lax.ppermute(lax.slice_in_dim(block, 0, width, axis=dim), axis, backward)
        block = jnp.concatenate([low, block, high], axis=dim)
    return block


def swapped(block, axis, apart):
    count = lax.axis_size(axis)
    route = []
    for low in range(count):
        high = low | 1 << apart
        if high != low and high < count:
            route += [(low, high), (high, low)]
    return lax.ppermute(block, axis, route)


def xor_partners(block, axis, low_bit, width):
    count = lax.axis_size(axis)
    return [
        lax.ppermute(block, axis, [(i, i ^ k << low_bit) for i in range(count)])
        for k in range(1, 1 << width)
    ]


def tree_stages(axis):
    bits = lax.axis_size(axis).bit_length() - 1
    return [(low, min(2, bits - low)) for low in range(0, bits, 2)]


def tree_sum(block, axis):
    stages = []
    for low_bit, width in reversed(tree_stages(axis)):
        for part in xor_partners(block, axis, low_bit, width):
            block = block + part
        stages.append(block)
    return block, stages[0]


def merge_packed(parts):
    larger = parts[0][..., :1]
    for part in parts[1:]:
        larger = jnp.maximum(larger, part[..., :1])
    mixed = parts[0][..., 1:] * jnp.exp(parts[0][..., :1] - larger)
    for part in parts[1:]:
        mixed = mixed + part[..., 1:] * jnp.exp(part[..., :1] - larger)
    return jnp.concatenate([larger, mixed], axis=-1)


def tree_merge(packed, axis):
    for low_bit, width in tree_stages(axis):
        packed = merge_packed([packed] + xor_partners(packed, axis, low_bit, width))
    return packed


def local(
    residual_in,
    query_rows,
    key_rows,
    value_rows,
    rand_blocks,
    global_blocks,
    out_weight,
    norm_gain,
    up_weight,
    down_weight,
):
    tok_rows = query_rows.shape[0]
    local_width = query_rows.shape[1]
    heads_here = local_width // HD
    shard_count = lax.axis_size("seq")
    my_shard = lax.axis_index("seq")
    total_blocks = QB_DEV * shard_count
    score_scale = 1.0 / math.sqrt(HD)
    q_heads = query_rows.reshape(QB_DEV, BLK, heads_here, HD)
    key_heads = key_rows.reshape(tok_rows, heads_here, HD)
    value_heads = value_rows.reshape(tok_rows, heads_here, HD)
    kv_tokens = jnp.concatenate([key_heads, value_heads], axis=2)
    padded = with_halo(kv_tokens, (("seq", 0),), BLK)
    padded_blocks = padded.reshape(QB_DEV + 2, BLK, heads_here, 2 * HD).transpose(0, 2, 1, 3)
    own_blocks = padded_blocks[1:-1]
    window_kv = jnp.stack([padded_blocks[:-2], own_blocks, padded_blocks[2:]], axis=2)
    flat_kv = (
        kv_tokens.reshape(QB_DEV, BLK, heads_here, 2 * HD)
        .transpose(0, 2, 1, 3)
        .reshape(QB_DEV * heads_here, BLK, 2 * HD)
    )
    position = my_shard % GROUP
    group_base = my_shard - position
    slot_count = QB_DEV * heads_here * R
    capacity = slot_count // GROUP
    offsets_all = jnp.arange(GROUP, dtype=jnp.int32)
    slot_heads = jnp.arange(slot_count, dtype=jnp.int32) // R % heads_here
    cap_range = jnp.arange(capacity, dtype=jnp.int32)

    def requests_of(shard):
        request_rows = lax.dynamic_slice_in_dim(rand_blocks, shard * QB_DEV, QB_DEV, 0)
        return request_rows.reshape(slot_count)

    def payload_for(offset):
        requester = group_base + (position - offset) % GROUP
        wanted = requests_of(requester)
        from_me = wanted // QB_DEV == my_shard
        order_rank = jnp.cumsum(from_me.astype(jnp.int32)) - 1
        source = wanted % QB_DEV * heads_here + slot_heads
        pick_table = from_me[:, None] & (order_rank[:, None] == cap_range[None, :])
        chosen = jnp.sum(jnp.where(pick_table, source[:, None], 0), axis=0)
        return jnp.take(flat_kv, chosen, axis=0)

    my_requests = requests_of(my_shard)
    owner_offset = (my_requests // QB_DEV - group_base - position) % GROUP
    offset_hits = owner_offset[:, None] == offsets_all[None, :]
    rank_table = jnp.cumsum(offset_hits.astype(jnp.int32), axis=0) - 1
    my_rank = jnp.sum(jnp.where(offset_hits, rank_table, 0), axis=1)
    slot_index = owner_offset * capacity + my_rank
    sectioned = jax.vmap(payload_for)(offsets_all)
    shard_ids = range(shard_count)
    arrived = [sectioned[0]]
    for offset in range(1, GROUP):
        route = [(s, s - s % GROUP + (s % GROUP - offset) % GROUP) for s in shard_ids]
        arrived.append(lax.ppermute(sectioned[offset], "seq", route))
    received = jnp.stack(arrived, axis=0)
    random_kv = jnp.take(received.reshape(GROUP * capacity, BLK, 2 * HD), slot_index, axis=0)
    random_kv = random_kv.reshape(QB_DEV, heads_here, R, BLK, 2 * HD)
    packed = jnp.stack([query_rows, key_rows, value_rows], axis=0)
    contributions = []
    for which in range(GLOB):
        global_id = global_blocks[which]
        block_rows = lax.dynamic_slice_in_dim(packed, global_id % QB_DEV * BLK, BLK, 1)
        is_owner = global_id // QB_DEV == my_shard
        contributions.append(jnp.where(is_owner, block_rows, jnp.zeros_like(block_rows)))
    global_packed, first_stage = tree_sum(jnp.stack(contributions, axis=0), "seq")
    mp_index = lax.axis_index("mp")
    mp_route = [(0, 1), (1, 0)]
    half_width = residual_in.shape[1] // lax.axis_size("mp")
    other_index = 1 - mp_index
    their_down = lax.dynamic_slice_in_dim(down_weight, other_index * half_width, half_width, 1)
    _, late_up, late_down, late_out = lax.optimization_barrier(
        (first_stage, up_weight, their_down, out_weight)
    )
    other_up = lax.ppermute(late_up, "mp", mp_route)
    other_down = lax.ppermute(late_down, "mp", mp_route)
    other_weight = lax.ppermute(late_out, "mp", mp_route)
    global_q = global_packed[:, 0].reshape(GLOB, BLK, heads_here, HD)
    global_k = global_packed[:, 1].reshape(GLOB, BLK, heads_here, HD)
    global_v = global_packed[:, 2].reshape(GLOB, BLK, heads_here, HD)
    global_kv = jnp.concatenate([global_k, global_v], axis=3).transpose(2, 0, 1, 3)
    global_kv = jnp.broadcast_to(global_kv[None], (QB_DEV, heads_here, GLOB, BLK, 2 * HD))
    all_kv = jnp.concatenate([window_kv, random_kv, global_kv], axis=2)
    keys_all = all_kv[..., :HD]
    values_all = all_kv[..., HD:]
    scores = (
        jnp.einsum("bqhd,bhjkd->bhqjk", q_heads, keys_all, preferred_element_type=jnp.float32)
        * score_scale
    )
    block_global = my_shard * QB_DEV + jnp.arange(QB_DEV, dtype=jnp.int32)
    valid_cols = jnp.concatenate(
        [
            (block_global >= 1)[:, None],
            jnp.ones((QB_DEV, 1), dtype=bool),
            (block_global + 1 < total_blocks)[:, None],
            jnp.ones((QB_DEV, R + GLOB), dtype=bool),
        ],
        axis=1,
    )
    scores = jnp.where(valid_cols[:, None, None, :, None], scores, jnp.float32(-1e30))
    row_peak = jnp.max(scores, axis=(3, 4), keepdims=True)
    weights = jnp.exp(scores - row_peak)
    row_total = jnp.sum(weights, axis=(3, 4))
    mixed_sum = jnp.einsum(
        "bhqjk,bhjkd->bqhd",
        weights.astype(jnp.bfloat16),
        values_all,
        preferred_element_type=jnp.float32,
    )
    sparse_out = mixed_sum / row_total.transpose(0, 2, 1)[..., None]
    global_scores = (
        jnp.einsum("gqhd,thd->ghqt", global_q, key_heads, preferred_element_type=jnp.float32)
        * score_scale
    )
    seg_peak = jnp.max(global_scores, axis=3)
    seg_weights = jnp.exp(global_scores - seg_peak[..., None])
    seg_total = jnp.sum(seg_weights, axis=3)
    seg_acc = jnp.einsum(
        "ghqt,thd->ghqd",
        seg_weights.astype(jnp.bfloat16),
        value_heads,
        preferred_element_type=jnp.float32,
    )
    seg_packed = jnp.concatenate([seg_peak[..., None], seg_total[..., None], seg_acc], axis=-1)
    merged = tree_merge(seg_packed, "seq")
    global_out = merged[..., 2:] / merged[..., 1:2]
    attn_rows = sparse_out.reshape(tok_rows, local_width)
    for which in range(GLOB):
        global_id = global_blocks[which]
        start_row = global_id % QB_DEV * BLK
        current = lax.dynamic_slice_in_dim(attn_rows, start_row, BLK, 0)
        replacing = global_out[which].transpose(1, 0, 2).reshape(BLK, local_width)
        is_owner = global_id // QB_DEV == my_shard
        attn_rows = lax.dynamic_update_slice_in_dim(
            attn_rows, jnp.where(is_owner, replacing, current), start_row, 0
        )
    attention = attn_rows.astype(jnp.bfloat16)
    attention, other_up, other_down = lax.optimization_barrier((attention, other_up, other_down))
    other_attention = lax.ppermute(attention, "mp", mp_route)
    projected = jnp.dot(attention, out_weight, preferred_element_type=jnp.float32) + jnp.dot(
        other_attention, other_weight, preferred_element_type=jnp.float32
    )
    middle = (residual_in.astype(jnp.float32) + projected).astype(jnp.bfloat16)
    middle_own = lax.dynamic_slice_in_dim(middle, mp_index * half_width, half_width, 1)
    middle32 = middle.astype(jnp.float32)
    row_mean = jnp.mean(middle32, axis=1, keepdims=True)
    centered = middle32 - row_mean
    row_var = jnp.mean(centered * centered, axis=1, keepdims=True)
    normed = (centered * lax.rsqrt(row_var + 1e-05) * norm_gain).astype(jnp.bfloat16)
    own_down = lax.dynamic_slice_in_dim(down_weight, mp_index * half_width, half_width, 1)
    hidden_own = jax.nn.gelu(
        jnp.dot(normed, up_weight, preferred_element_type=jnp.float32), approximate=True
    ).astype(jnp.bfloat16)
    hidden_other = jax.nn.gelu(
        jnp.dot(normed, other_up, preferred_element_type=jnp.float32), approximate=True
    ).astype(jnp.bfloat16)
    down_part = jnp.dot(hidden_own, own_down, preferred_element_type=jnp.float32) + jnp.dot(
        hidden_other, other_down, preferred_element_type=jnp.float32
    )
    return (middle_own.astype(jnp.float32) + down_part).astype(jnp.bfloat16)


def solution(mesh):
    placed = (
        P("seq", None),
        P("seq", "mp"),
        P("seq", "mp"),
        P("seq", "mp"),
        P(None, "mp", None),
        P(),
        P("mp", None),
        P(),
        P(None, "mp"),
        P("mp", None),
    )
    return jax.shard_map(
        local, mesh=mesh, in_specs=placed, out_specs=P("seq", "mp"), check_vma=False
    )
```

```python
import math

import jax
import jax.numpy as jnp
from jax import lax
from jax.sharding import PartitionSpec as P

HD = 64
BLK = 64
R = 3
GLOB = 2
GROUP = 16
QB_DEV = 16


def with_halo(block, sides, width):
    for axis, dim in sides:
        count = lax.axis_size(axis)
        forward = [(i, i + 1) for i in range(count - 1)]
        backward = [(target, source) for source, target in forward]
        low = lax.ppermute(
            lax.slice_in_dim(block, block.shape[dim] - width, None, axis=dim), axis, forward
        )
        high = lax.ppermute(lax.slice_in_dim(block, 0, width, axis=dim), axis, backward)
        block = jnp.concatenate([low, block, high], axis=dim)
    return block


def swapped(block, axis, apart):
    count = lax.axis_size(axis)
    route = []
    for low in range(count):
        high = low | 1 << apart
        if high != low and high < count:
            route += [(low, high), (high, low)]
    return lax.ppermute(block, axis, route)


def xor_partners(block, axis, low_bit, width):
    count = lax.axis_size(axis)
    return [
        lax.ppermute(block, axis, [(i, i ^ k << low_bit) for i in range(count)])
        for k in range(1, 1 << width)
    ]


def tree_stages(axis):
    bits = lax.axis_size(axis).bit_length() - 1
    return [(low, min(2, bits - low)) for low in range(0, bits, 2)]


def tree_sum(block, axis):
    stages = []
    for low_bit, width in reversed(tree_stages(axis)):
        for part in xor_partners(block, axis, low_bit, width):
            block = block + part
        stages.append(block)
    return block, stages


def merge_packed(parts):
    larger = parts[0][..., :1]
    for part in parts[1:]:
        larger = jnp.maximum(larger, part[..., :1])
    mixed = parts[0][..., 1:] * jnp.exp(parts[0][..., :1] - larger)
    for part in parts[1:]:
        mixed = mixed + part[..., 1:] * jnp.exp(part[..., :1] - larger)
    return jnp.concatenate([larger, mixed], axis=-1)


def tree_merge(packed, axis):
    for low_bit, width in tree_stages(axis):
        packed = merge_packed([packed] + xor_partners(packed, axis, low_bit, width))
    return packed


def local(
    residual_in,
    query_rows,
    key_rows,
    value_rows,
    rand_blocks,
    global_blocks,
    out_weight,
    norm_gain,
    up_weight,
    down_weight,
):
    tok_rows = query_rows.shape[0]
    local_width = query_rows.shape[1]
    heads_here = local_width // HD
    shard_count = lax.axis_size("seq")
    my_shard = lax.axis_index("seq")
    total_blocks = QB_DEV * shard_count
    score_scale = 1.0 / math.sqrt(HD)
    q_heads = query_rows.reshape(QB_DEV, BLK, heads_here, HD)
    key_heads = key_rows.reshape(tok_rows, heads_here, HD)
    value_heads = value_rows.reshape(tok_rows, heads_here, HD)
    kv_tokens = jnp.concatenate([key_heads, value_heads], axis=2)
    padded = with_halo(kv_tokens, (("seq", 0),), BLK)
    padded_blocks = padded.reshape(QB_DEV + 2, BLK, heads_here, 2 * HD).transpose(0, 2, 1, 3)
    own_blocks = padded_blocks[1:-1]
    window_kv = jnp.stack([padded_blocks[:-2], own_blocks, padded_blocks[2:]], axis=2)
    flat_kv = (
        kv_tokens.reshape(QB_DEV, BLK, heads_here, 2 * HD)
        .transpose(0, 2, 1, 3)
        .reshape(QB_DEV * heads_here, BLK, 2 * HD)
    )
    position = my_shard % GROUP
    group_base = my_shard - position
    slot_count = QB_DEV * heads_here * R
    capacity = slot_count // GROUP
    offsets_all = jnp.arange(GROUP, dtype=jnp.int32)
    slot_heads = jnp.arange(slot_count, dtype=jnp.int32) // R % heads_here
    cap_range = jnp.arange(capacity, dtype=jnp.int32)

    def requests_of(shard):
        request_rows = lax.dynamic_slice_in_dim(rand_blocks, shard * QB_DEV, QB_DEV, 0)
        return request_rows.reshape(slot_count)

    def payload_for(offset):
        requester = group_base + (position - offset) % GROUP
        wanted = requests_of(requester)
        from_me = wanted // QB_DEV == my_shard
        order_rank = jnp.cumsum(from_me.astype(jnp.int32)) - 1
        source = wanted % QB_DEV * heads_here + slot_heads
        pick_table = from_me[:, None] & (order_rank[:, None] == cap_range[None, :])
        chosen = jnp.sum(jnp.where(pick_table, source[:, None], 0), axis=0)
        return jnp.take(flat_kv, chosen, axis=0)

    my_requests = requests_of(my_shard)
    owner_offset = (my_requests // QB_DEV - group_base - position) % GROUP
    offset_hits = owner_offset[:, None] == offsets_all[None, :]
    rank_table = jnp.cumsum(offset_hits.astype(jnp.int32), axis=0) - 1
    my_rank = jnp.sum(jnp.where(offset_hits, rank_table, 0), axis=1)
    slot_index = owner_offset * capacity + my_rank
    sectioned = jax.vmap(payload_for)(offsets_all)
    packed = jnp.stack([query_rows, key_rows, value_rows], axis=0)
    contributions = []
    for which in range(GLOB):
        global_id = global_blocks[which]
        block_rows = lax.dynamic_slice_in_dim(packed, global_id % QB_DEV * BLK, BLK, 1)
        is_owner = global_id // QB_DEV == my_shard
        contributions.append(jnp.where(is_owner, block_rows, jnp.zeros_like(block_rows)))
    global_packed, tree_steps = tree_sum(jnp.stack(contributions, axis=0), "seq")
    mp_index = lax.axis_index("mp")
    mp_route = [(0, 1), (1, 0)]
    half_width = residual_in.shape[1] // lax.axis_size("mp")
    other_index = 1 - mp_index
    their_down = lax.dynamic_slice_in_dim(down_weight, other_index * half_width, half_width, 1)
    _, late_up, late_down, late_out = lax.optimization_barrier(
        (tree_steps[0], up_weight, their_down, out_weight)
    )
    other_up = lax.ppermute(late_up, "mp", mp_route)
    other_down = lax.ppermute(late_down, "mp", mp_route)
    other_weight = lax.ppermute(late_out, "mp", mp_route)
    sectioned, _ = lax.optimization_barrier((sectioned, tree_steps[1]))
    shard_ids = range(shard_count)
    arrived = [sectioned[0]]
    for offset in range(1, GROUP):
        route = [(s, s - s % GROUP + (s % GROUP - offset) % GROUP) for s in shard_ids]
        arrived.append(lax.ppermute(sectioned[offset], "seq", route))
    received = jnp.stack(arrived, axis=0)
    random_kv = jnp.take(received.reshape(GROUP * capacity, BLK, 2 * HD), slot_index, axis=0)
    random_kv = random_kv.reshape(QB_DEV, heads_here, R, BLK, 2 * HD)
    global_q = global_packed[:, 0].reshape(GLOB, BLK, heads_here, HD)
    global_k = global_packed[:, 1].reshape(GLOB, BLK, heads_here, HD)
    global_v = global_packed[:, 2].reshape(GLOB, BLK, heads_here, HD)
    global_kv = jnp.concatenate([global_k, global_v], axis=3).transpose(2, 0, 1, 3)
    global_kv = jnp.broadcast_to(global_kv[None], (QB_DEV, heads_here, GLOB, BLK, 2 * HD))
    all_kv = jnp.concatenate([window_kv, random_kv, global_kv], axis=2)
    keys_all = all_kv[..., :HD]
    values_all = all_kv[..., HD:]
    scores = (
        jnp.einsum("bqhd,bhjkd->bhqjk", q_heads, keys_all, preferred_element_type=jnp.float32)
        * score_scale
    )
    block_global = my_shard * QB_DEV + jnp.arange(QB_DEV, dtype=jnp.int32)
    valid_cols = jnp.concatenate(
        [
            (block_global >= 1)[:, None],
            jnp.ones((QB_DEV, 1), dtype=bool),
            (block_global + 1 < total_blocks)[:, None],
            jnp.ones((QB_DEV, R + GLOB), dtype=bool),
        ],
        axis=1,
    )
    scores = jnp.where(valid_cols[:, None, None, :, None], scores, jnp.float32(-1e30))
    row_peak = jnp.max(scores, axis=(3, 4), keepdims=True)
    weights = jnp.exp(scores - row_peak)
    row_total = jnp.sum(weights, axis=(3, 4))
    mixed_sum = jnp.einsum(
        "bhqjk,bhjkd->bqhd",
        weights.astype(jnp.bfloat16),
        values_all,
        preferred_element_type=jnp.float32,
    )
    sparse_out = mixed_sum / row_total.transpose(0, 2, 1)[..., None]
    global_scores = (
        jnp.einsum("gqhd,thd->ghqt", global_q, key_heads, preferred_element_type=jnp.float32)
        * score_scale
    )
    seg_peak = jnp.max(global_scores, axis=3)
    seg_weights = jnp.exp(global_scores - seg_peak[..., None])
    seg_total = jnp.sum(seg_weights, axis=3)
    seg_acc = jnp.einsum(
        "ghqt,thd->ghqd",
        seg_weights.astype(jnp.bfloat16),
        value_heads,
        preferred_element_type=jnp.float32,
    )
    seg_packed = jnp.concatenate([seg_peak[..., None], seg_total[..., None], seg_acc], axis=-1)
    merged = tree_merge(seg_packed, "seq")
    global_out = merged[..., 2:] / merged[..., 1:2]
    attn_rows = sparse_out.reshape(tok_rows, local_width)
    for which in range(GLOB):
        global_id = global_blocks[which]
        start_row = global_id % QB_DEV * BLK
        current = lax.dynamic_slice_in_dim(attn_rows, start_row, BLK, 0)
        replacing = global_out[which].transpose(1, 0, 2).reshape(BLK, local_width)
        is_owner = global_id // QB_DEV == my_shard
        attn_rows = lax.dynamic_update_slice_in_dim(
            attn_rows, jnp.where(is_owner, replacing, current), start_row, 0
        )
    attention = attn_rows.astype(jnp.bfloat16)
    attention, other_up, other_down = lax.optimization_barrier((attention, other_up, other_down))
    other_attention = lax.ppermute(attention, "mp", mp_route)
    projected = jnp.dot(attention, out_weight, preferred_element_type=jnp.float32) + jnp.dot(
        other_attention, other_weight, preferred_element_type=jnp.float32
    )
    middle = (residual_in.astype(jnp.float32) + projected).astype(jnp.bfloat16)
    middle_own = lax.dynamic_slice_in_dim(middle, mp_index * half_width, half_width, 1)
    middle32 = middle.astype(jnp.float32)
    row_mean = jnp.mean(middle32, axis=1, keepdims=True)
    centered = middle32 - row_mean
    row_var = jnp.mean(centered * centered, axis=1, keepdims=True)
    normed = (centered * lax.rsqrt(row_var + 1e-05) * norm_gain).astype(jnp.bfloat16)
    own_down = lax.dynamic_slice_in_dim(down_weight, mp_index * half_width, half_width, 1)
    hidden_own = jax.nn.gelu(
        jnp.dot(normed, up_weight, preferred_element_type=jnp.float32), approximate=True
    ).astype(jnp.bfloat16)
    hidden_other = jax.nn.gelu(
        jnp.dot(normed, other_up, preferred_element_type=jnp.float32), approximate=True
    ).astype(jnp.bfloat16)
    down_part = jnp.dot(hidden_own, own_down, preferred_element_type=jnp.float32) + jnp.dot(
        hidden_other, other_down, preferred_element_type=jnp.float32
    )
    return (middle_own.astype(jnp.float32) + down_part).astype(jnp.bfloat16)


def solution(mesh):
    placed = (
        P("seq", None),
        P("seq", "mp"),
        P("seq", "mp"),
        P("seq", "mp"),
        P(None, "mp", None),
        P(),
        P("mp", None),
        P(),
        P(None, "mp"),
        P("mp", None),
    )
    return jax.shard_map(
        local, mesh=mesh, in_specs=placed, out_specs=P("seq", "mp"), check_vma=False
    )
```

```python
import math

import jax
import jax.numpy as jnp
from jax import lax
from jax.sharding import PartitionSpec as P

HD = 64
BLK = 64
R = 3
GLOB = 2
GROUP = 16
QB_DEV = 16


def with_halo(block, sides, width):
    for axis, dim in sides:
        count = lax.axis_size(axis)
        forward = [(i, i + 1) for i in range(count - 1)]
        backward = [(target, source) for source, target in forward]
        low = lax.ppermute(
            lax.slice_in_dim(block, block.shape[dim] - width, None, axis=dim), axis, forward
        )
        high = lax.ppermute(lax.slice_in_dim(block, 0, width, axis=dim), axis, backward)
        block = jnp.concatenate([low, block, high], axis=dim)
    return block


def swapped(block, axis, apart):
    count = lax.axis_size(axis)
    route = []
    for low in range(count):
        high = low | 1 << apart
        if high != low and high < count:
            route += [(low, high), (high, low)]
    return lax.ppermute(block, axis, route)


def xor_partners(block, axis, low_bit, width):
    count = lax.axis_size(axis)
    return [
        lax.ppermute(block, axis, [(i, i ^ k << low_bit) for i in range(count)])
        for k in range(1, 1 << width)
    ]


def tree_stages(axis):
    bits = lax.axis_size(axis).bit_length() - 1
    return [(low, min(2, bits - low)) for low in range(0, bits, 2)]


def tree_sum(block, axis):
    stages = []
    for low_bit, width in reversed(tree_stages(axis)):
        for part in xor_partners(block, axis, low_bit, width):
            block = block + part
        stages.append(block)
    return block, stages


def merge_packed(parts):
    larger = parts[0][..., :1]
    for part in parts[1:]:
        larger = jnp.maximum(larger, part[..., :1])
    mixed = parts[0][..., 1:] * jnp.exp(parts[0][..., :1] - larger)
    for part in parts[1:]:
        mixed = mixed + part[..., 1:] * jnp.exp(part[..., :1] - larger)
    return jnp.concatenate([larger, mixed], axis=-1)


def tree_merge(packed, axis):
    for low_bit, width in tree_stages(axis):
        packed = merge_packed([packed] + xor_partners(packed, axis, low_bit, width))
    return packed


def local(
    residual_in,
    query_rows,
    key_rows,
    value_rows,
    rand_blocks,
    global_blocks,
    out_weight,
    norm_gain,
    up_weight,
    down_weight,
):
    tok_rows = query_rows.shape[0]
    local_width = query_rows.shape[1]
    heads_here = local_width // HD
    shard_count = lax.axis_size("seq")
    my_shard = lax.axis_index("seq")
    total_blocks = QB_DEV * shard_count
    score_scale = 1.0 / math.sqrt(HD)
    q_heads = query_rows.reshape(QB_DEV, BLK, heads_here, HD)
    key_heads = key_rows.reshape(tok_rows, heads_here, HD)
    value_heads = value_rows.reshape(tok_rows, heads_here, HD)
    kv_tokens = jnp.concatenate([key_heads, value_heads], axis=2)
    padded = with_halo(kv_tokens, (("seq", 0),), BLK)
    padded_blocks = padded.reshape(QB_DEV + 2, BLK, heads_here, 2 * HD).transpose(0, 2, 1, 3)
    own_blocks = padded_blocks[1:-1]
    window_kv = jnp.stack([padded_blocks[:-2], own_blocks, padded_blocks[2:]], axis=2)
    flat_kv = (
        kv_tokens.reshape(QB_DEV, BLK, heads_here, 2 * HD)
        .transpose(0, 2, 1, 3)
        .reshape(QB_DEV * heads_here, BLK, 2 * HD)
    )
    position = my_shard % GROUP
    group_base = my_shard - position
    slot_count = QB_DEV * heads_here * R
    capacity = slot_count // GROUP
    offsets_all = jnp.arange(GROUP, dtype=jnp.int32)
    slot_heads = jnp.arange(slot_count, dtype=jnp.int32) // R % heads_here
    cap_range = jnp.arange(capacity, dtype=jnp.int32)

    def requests_of(shard):
        request_rows = lax.dynamic_slice_in_dim(rand_blocks, shard * QB_DEV, QB_DEV, 0)
        return request_rows.reshape(slot_count)

    def payload_for(offset):
        requester = group_base + (position - offset) % GROUP
        wanted = requests_of(requester)
        from_me = wanted // QB_DEV == my_shard
        order_rank = jnp.cumsum(from_me.astype(jnp.int32)) - 1
        source = wanted % QB_DEV * heads_here + slot_heads
        pick_table = from_me[:, None] & (order_rank[:, None] == cap_range[None, :])
        chosen = jnp.sum(jnp.where(pick_table, source[:, None], 0), axis=0)
        return jnp.take(flat_kv, chosen, axis=0)

    my_requests = requests_of(my_shard)
    owner_offset = (my_requests // QB_DEV - group_base - position) % GROUP
    offset_hits = owner_offset[:, None] == offsets_all[None, :]
    rank_table = jnp.cumsum(offset_hits.astype(jnp.int32), axis=0) - 1
    my_rank = jnp.sum(jnp.where(offset_hits, rank_table, 0), axis=1)
    slot_index = owner_offset * capacity + my_rank
    sectioned = jax.vmap(payload_for)(offsets_all)
    packed = jnp.stack([query_rows, key_rows, value_rows], axis=0)
    contributions = []
    for which in range(GLOB):
        global_id = global_blocks[which]
        block_rows = lax.dynamic_slice_in_dim(packed, global_id % QB_DEV * BLK, BLK, 1)
        is_owner = global_id // QB_DEV == my_shard
        contributions.append(jnp.where(is_owner, block_rows, jnp.zeros_like(block_rows)))
    global_packed, tree_steps = tree_sum(jnp.stack(contributions, axis=0), "seq")
    mp_index = lax.axis_index("mp")
    mp_route = [(0, 1), (1, 0)]
    half_width = residual_in.shape[1] // lax.axis_size("mp")
    other_index = 1 - mp_index
    their_down = lax.dynamic_slice_in_dim(down_weight, other_index * half_width, half_width, 1)
    _, late_up, late_down, late_out = lax.optimization_barrier(
        (tree_steps[0], up_weight, their_down, out_weight)
    )
    other_up = lax.ppermute(late_up, "mp", mp_route)
    other_down = lax.ppermute(late_down, "mp", mp_route)
    other_weight = lax.ppermute(late_out, "mp", mp_route)
    sectioned, _ = lax.optimization_barrier((sectioned, tree_steps[0]))
    shard_ids = range(shard_count)
    arrived = [sectioned[0]]
    for offset in range(1, GROUP):
        route = [(s, s - s % GROUP + (s % GROUP - offset) % GROUP) for s in shard_ids]
        arrived.append(lax.ppermute(sectioned[offset], "seq", route))
    received = jnp.stack(arrived, axis=0)
    random_kv = jnp.take(received.reshape(GROUP * capacity, BLK, 2 * HD), slot_index, axis=0)
    random_kv = random_kv.reshape(QB_DEV, heads_here, R, BLK, 2 * HD)
    global_q = global_packed[:, 0].reshape(GLOB, BLK, heads_here, HD)
    global_k = global_packed[:, 1].reshape(GLOB, BLK, heads_here, HD)
    global_v = global_packed[:, 2].reshape(GLOB, BLK, heads_here, HD)
    global_kv = jnp.concatenate([global_k, global_v], axis=3).transpose(2, 0, 1, 3)
    global_kv = jnp.broadcast_to(global_kv[None], (QB_DEV, heads_here, GLOB, BLK, 2 * HD))
    all_kv = jnp.concatenate([window_kv, random_kv, global_kv], axis=2)
    keys_all = all_kv[..., :HD]
    values_all = all_kv[..., HD:]
    scores = (
        jnp.einsum("bqhd,bhjkd->bhqjk", q_heads, keys_all, preferred_element_type=jnp.float32)
        * score_scale
    )
    block_global = my_shard * QB_DEV + jnp.arange(QB_DEV, dtype=jnp.int32)
    valid_cols = jnp.concatenate(
        [
            (block_global >= 1)[:, None],
            jnp.ones((QB_DEV, 1), dtype=bool),
            (block_global + 1 < total_blocks)[:, None],
            jnp.ones((QB_DEV, R + GLOB), dtype=bool),
        ],
        axis=1,
    )
    scores = jnp.where(valid_cols[:, None, None, :, None], scores, jnp.float32(-1e30))
    row_peak = jnp.max(scores, axis=(3, 4), keepdims=True)
    weights = jnp.exp(scores - row_peak)
    row_total = jnp.sum(weights, axis=(3, 4))
    mixed_sum = jnp.einsum(
        "bhqjk,bhjkd->bqhd",
        weights.astype(jnp.bfloat16),
        values_all,
        preferred_element_type=jnp.float32,
    )
    sparse_out = mixed_sum / row_total.transpose(0, 2, 1)[..., None]
    global_scores = (
        jnp.einsum("gqhd,thd->ghqt", global_q, key_heads, preferred_element_type=jnp.float32)
        * score_scale
    )
    seg_peak = jnp.max(global_scores, axis=3)
    seg_weights = jnp.exp(global_scores - seg_peak[..., None])
    seg_total = jnp.sum(seg_weights, axis=3)
    seg_acc = jnp.einsum(
        "ghqt,thd->ghqd",
        seg_weights.astype(jnp.bfloat16),
        value_heads,
        preferred_element_type=jnp.float32,
    )
    seg_packed = jnp.concatenate([seg_peak[..., None], seg_total[..., None], seg_acc], axis=-1)
    merged = tree_merge(seg_packed, "seq")
    global_out = merged[..., 2:] / merged[..., 1:2]
    attn_rows = sparse_out.reshape(tok_rows, local_width)
    for which in range(GLOB):
        global_id = global_blocks[which]
        start_row = global_id % QB_DEV * BLK
        current = lax.dynamic_slice_in_dim(attn_rows, start_row, BLK, 0)
        replacing = global_out[which].transpose(1, 0, 2).reshape(BLK, local_width)
        is_owner = global_id // QB_DEV == my_shard
        attn_rows = lax.dynamic_update_slice_in_dim(
            attn_rows, jnp.where(is_owner, replacing, current), start_row, 0
        )
    attention = attn_rows.astype(jnp.bfloat16)
    attention, other_up, other_down = lax.optimization_barrier((attention, other_up, other_down))
    other_attention = lax.ppermute(attention, "mp", mp_route)
    projected = jnp.dot(attention, out_weight, preferred_element_type=jnp.float32) + jnp.dot(
        other_attention, other_weight, preferred_element_type=jnp.float32
    )
    middle = (residual_in.astype(jnp.float32) + projected).astype(jnp.bfloat16)
    middle_own = lax.dynamic_slice_in_dim(middle, mp_index * half_width, half_width, 1)
    middle32 = middle.astype(jnp.float32)
    row_mean = jnp.mean(middle32, axis=1, keepdims=True)
    centered = middle32 - row_mean
    row_var = jnp.mean(centered * centered, axis=1, keepdims=True)
    normed = (centered * lax.rsqrt(row_var + 1e-05) * norm_gain).astype(jnp.bfloat16)
    own_down = lax.dynamic_slice_in_dim(down_weight, mp_index * half_width, half_width, 1)
    hidden_own = jax.nn.gelu(
        jnp.dot(normed, up_weight, preferred_element_type=jnp.float32), approximate=True
    ).astype(jnp.bfloat16)
    hidden_other = jax.nn.gelu(
        jnp.dot(normed, other_up, preferred_element_type=jnp.float32), approximate=True
    ).astype(jnp.bfloat16)
    down_part = jnp.dot(hidden_own, own_down, preferred_element_type=jnp.float32) + jnp.dot(
        hidden_other, other_down, preferred_element_type=jnp.float32
    )
    return (middle_own.astype(jnp.float32) + down_part).astype(jnp.bfloat16)


def solution(mesh):
    placed = (
        P("seq", None),
        P("seq", "mp"),
        P("seq", "mp"),
        P("seq", "mp"),
        P(None, "mp", None),
        P(),
        P("mp", None),
        P(),
        P(None, "mp"),
        P("mp", None),
    )
    return jax.shard_map(
        local, mesh=mesh, in_specs=placed, out_specs=P("seq", "mp"), check_vma=False
    )
```

```python
import math

import jax
import jax.numpy as jnp
from jax import lax
from jax.sharding import PartitionSpec as P

HD = 64
BLK = 64
R = 3
GLOB = 2
GROUP = 16
QB_DEV = 16


def with_halo(block, sides, width):
    for axis, dim in sides:
        count = lax.axis_size(axis)
        forward = [(i, i + 1) for i in range(count - 1)]
        backward = [(target, source) for source, target in forward]
        low = lax.ppermute(
            lax.slice_in_dim(block, block.shape[dim] - width, None, axis=dim), axis, forward
        )
        high = lax.ppermute(lax.slice_in_dim(block, 0, width, axis=dim), axis, backward)
        block = jnp.concatenate([low, block, high], axis=dim)
    return block


def swapped(block, axis, apart):
    count = lax.axis_size(axis)
    route = []
    for low in range(count):
        high = low | 1 << apart
        if high != low and high < count:
            route += [(low, high), (high, low)]
    return lax.ppermute(block, axis, route)


def xor_partners(block, axis, low_bit, width):
    count = lax.axis_size(axis)
    return [
        lax.ppermute(block, axis, [(i, i ^ k << low_bit) for i in range(count)])
        for k in range(1, 1 << width)
    ]


def tree_stages(axis):
    bits = lax.axis_size(axis).bit_length() - 1
    return [(low, min(2, bits - low)) for low in range(0, bits, 2)]


def tree_sum(block, axis):
    for low_bit, width in tree_stages(axis):
        for part in xor_partners(block, axis, low_bit, width):
            block = block + part
    return block


def merge_packed(parts):
    larger = parts[0][..., :1]
    for part in parts[1:]:
        larger = jnp.maximum(larger, part[..., :1])
    mixed = parts[0][..., 1:] * jnp.exp(parts[0][..., :1] - larger)
    for part in parts[1:]:
        mixed = mixed + part[..., 1:] * jnp.exp(part[..., :1] - larger)
    return jnp.concatenate([larger, mixed], axis=-1)


def tree_merge(packed, axis):
    for low_bit, width in tree_stages(axis):
        packed = merge_packed([packed] + xor_partners(packed, axis, low_bit, width))
    return packed


def local(
    residual_in,
    query_rows,
    key_rows,
    value_rows,
    rand_blocks,
    global_blocks,
    out_weight,
    norm_gain,
    up_weight,
    down_weight,
):
    tok_rows = query_rows.shape[0]
    local_width = query_rows.shape[1]
    heads_here = local_width // HD
    shard_count = lax.axis_size("seq")
    my_shard = lax.axis_index("seq")
    total_blocks = QB_DEV * shard_count
    score_scale = 1.0 / math.sqrt(HD)
    q_heads = query_rows.reshape(QB_DEV, BLK, heads_here, HD)
    key_heads = key_rows.reshape(tok_rows, heads_here, HD)
    value_heads = value_rows.reshape(tok_rows, heads_here, HD)
    kv_tokens = jnp.concatenate([key_heads, value_heads], axis=2)
    padded = with_halo(kv_tokens, (("seq", 0),), BLK)
    padded_blocks = padded.reshape(QB_DEV + 2, BLK, heads_here, 2 * HD).transpose(0, 2, 1, 3)
    own_blocks = padded_blocks[1:-1]
    window_kv = jnp.stack([padded_blocks[:-2], own_blocks, padded_blocks[2:]], axis=2)
    flat_kv = own_blocks.reshape(QB_DEV * heads_here, BLK, 2 * HD)
    position = my_shard % GROUP
    group_base = my_shard - position
    slot_count = QB_DEV * heads_here * R
    capacity = slot_count // GROUP
    offsets_all = jnp.arange(GROUP, dtype=jnp.int32)
    slot_heads = jnp.arange(slot_count, dtype=jnp.int32) // R % heads_here
    cap_range = jnp.arange(capacity, dtype=jnp.int32)

    def requests_of(shard):
        request_rows = lax.dynamic_slice_in_dim(rand_blocks, shard * QB_DEV, QB_DEV, 0)
        return request_rows.reshape(slot_count)

    def payload_for(offset):
        requester = group_base + (position - offset) % GROUP
        wanted = requests_of(requester)
        from_me = wanted // QB_DEV == my_shard
        order_rank = jnp.cumsum(from_me.astype(jnp.int32)) - 1
        source = wanted % QB_DEV * heads_here + slot_heads
        pick_table = from_me[:, None] & (order_rank[:, None] == cap_range[None, :])
        chosen = jnp.sum(jnp.where(pick_table, source[:, None], 0), axis=0)
        return jnp.take(flat_kv, chosen, axis=0)

    my_requests = requests_of(my_shard)
    owner_offset = (my_requests // QB_DEV - group_base - position) % GROUP
    offset_hits = owner_offset[:, None] == offsets_all[None, :]
    rank_table = jnp.cumsum(offset_hits.astype(jnp.int32), axis=0) - 1
    my_rank = jnp.sum(jnp.where(offset_hits, rank_table, 0), axis=1)
    slot_index = owner_offset * capacity + my_rank
    sectioned = jax.vmap(payload_for)(offsets_all)
    shard_ids = range(shard_count)
    arrived = [sectioned[0]]
    for offset in range(1, GROUP):
        route = [(s, s - s % GROUP + (s % GROUP - offset) % GROUP) for s in shard_ids]
        arrived.append(lax.ppermute(sectioned[offset], "seq", route))
    received = jnp.stack(arrived, axis=0)
    random_kv = jnp.take(received.reshape(GROUP * capacity, BLK, 2 * HD), slot_index, axis=0)
    random_kv = random_kv.reshape(QB_DEV, heads_here, R, BLK, 2 * HD)
    packed = jnp.stack([query_rows, key_rows, value_rows], axis=0)
    contributions = []
    for which in range(GLOB):
        global_id = global_blocks[which]
        block_rows = lax.dynamic_slice_in_dim(packed, global_id % QB_DEV * BLK, BLK, 1)
        is_owner = global_id // QB_DEV == my_shard
        contributions.append(jnp.where(is_owner, block_rows, jnp.zeros_like(block_rows)))
    global_packed = tree_sum(jnp.stack(contributions, axis=0), "seq")
    global_q = global_packed[:, 0].reshape(GLOB, BLK, heads_here, HD)
    global_k = global_packed[:, 1].reshape(GLOB, BLK, heads_here, HD)
    global_v = global_packed[:, 2].reshape(GLOB, BLK, heads_here, HD)
    global_kv = jnp.concatenate([global_k, global_v], axis=3).transpose(2, 0, 1, 3)
    global_kv = jnp.broadcast_to(global_kv[None], (QB_DEV, heads_here, GLOB, BLK, 2 * HD))
    all_kv = jnp.concatenate([window_kv, random_kv, global_kv], axis=2)
    keys_all = all_kv[..., :HD]
    values_all = all_kv[..., HD:]
    scores = (
        jnp.einsum("bqhd,bhjkd->bhqjk", q_heads, keys_all, preferred_element_type=jnp.float32)
        * score_scale
    )
    block_global = my_shard * QB_DEV + jnp.arange(QB_DEV, dtype=jnp.int32)
    valid_cols = jnp.concatenate(
        [
            (block_global >= 1)[:, None],
            jnp.ones((QB_DEV, 1), dtype=bool),
            (block_global + 1 < total_blocks)[:, None],
            jnp.ones((QB_DEV, R + GLOB), dtype=bool),
        ],
        axis=1,
    )
    scores = jnp.where(valid_cols[:, None, None, :, None], scores, jnp.float32(-1e30))
    row_peak = jnp.max(scores, axis=(3, 4), keepdims=True)
    weights = jnp.exp(scores - row_peak)
    row_total = jnp.sum(weights, axis=(3, 4))
    mixed_sum = jnp.einsum(
        "bhqjk,bhjkd->bqhd",
        weights.astype(jnp.bfloat16),
        values_all,
        preferred_element_type=jnp.float32,
    )
    sparse_out = mixed_sum / row_total.transpose(0, 2, 1)[..., None]
    global_scores = (
        jnp.einsum("gqhd,thd->ghqt", global_q, key_heads, preferred_element_type=jnp.float32)
        * score_scale
    )
    seg_peak = jnp.max(global_scores, axis=3)
    seg_weights = jnp.exp(global_scores - seg_peak[..., None])
    seg_total = jnp.sum(seg_weights, axis=3)
    seg_acc = jnp.einsum(
        "ghqt,thd->ghqd",
        seg_weights.astype(jnp.bfloat16),
        value_heads,
        preferred_element_type=jnp.float32,
    )
    mp_index = lax.axis_index("mp")
    mp_route = [(0, 1), (1, 0)]
    half_width = residual_in.shape[1] // lax.axis_size("mp")
    other_up = lax.ppermute(up_weight, "mp", mp_route)
    other_index = 1 - mp_index
    their_down = lax.dynamic_slice_in_dim(down_weight, other_index * half_width, half_width, 1)
    other_down = lax.ppermute(their_down, "mp", mp_route)
    seg_packed = jnp.concatenate([seg_peak[..., None], seg_total[..., None], seg_acc], axis=-1)
    seg_packed, other_up, other_down = lax.optimization_barrier((seg_packed, other_up, other_down))
    merged = tree_merge(seg_packed, "seq")
    global_out = merged[..., 2:] / merged[..., 1:2]
    attn_rows = sparse_out.reshape(tok_rows, local_width)
    for which in range(GLOB):
        global_id = global_blocks[which]
        start_row = global_id % QB_DEV * BLK
        current = lax.dynamic_slice_in_dim(attn_rows, start_row, BLK, 0)
        replacing = global_out[which].transpose(1, 0, 2).reshape(BLK, local_width)
        is_owner = global_id // QB_DEV == my_shard
        attn_rows = lax.dynamic_update_slice_in_dim(
            attn_rows, jnp.where(is_owner, replacing, current), start_row, 0
        )
    attention = attn_rows.astype(jnp.bfloat16)
    other_weight = lax.ppermute(out_weight, "mp", mp_route)
    own_down = lax.dynamic_slice_in_dim(down_weight, mp_index * half_width, half_width, 1)
    chunk_rows = tok_rows // 2
    results = []
    for first_row in range(0, tok_rows, chunk_rows):
        mine = lax.slice_in_dim(attention, first_row, first_row + chunk_rows, axis=0)
        theirs = lax.ppermute(mine, "mp", mp_route)
        projected = jnp.dot(mine, out_weight, preferred_element_type=jnp.float32) + jnp.dot(
            theirs, other_weight, preferred_element_type=jnp.float32
        )
        residual = lax.slice_in_dim(residual_in, first_row, first_row + chunk_rows, axis=0)
        middle = (residual.astype(jnp.float32) + projected).astype(jnp.bfloat16)
        middle_own = lax.dynamic_slice_in_dim(middle, mp_index * half_width, half_width, 1)
        middle32 = middle.astype(jnp.float32)
        row_mean = jnp.mean(middle32, axis=1, keepdims=True)
        centered = middle32 - row_mean
        row_var = jnp.mean(centered * centered, axis=1, keepdims=True)
        normed = (centered * lax.rsqrt(row_var + 1e-05) * norm_gain).astype(jnp.bfloat16)
        hidden_own = jax.nn.gelu(
            jnp.dot(normed, up_weight, preferred_element_type=jnp.float32), approximate=True
        ).astype(jnp.bfloat16)
        hidden_other = jax.nn.gelu(
            jnp.dot(normed, other_up, preferred_element_type=jnp.float32), approximate=True
        ).astype(jnp.bfloat16)
        down_part = jnp.dot(hidden_own, own_down, preferred_element_type=jnp.float32) + jnp.dot(
            hidden_other, other_down, preferred_element_type=jnp.float32
        )
        results.append((middle_own.astype(jnp.float32) + down_part).astype(jnp.bfloat16))
    return jnp.concatenate(results, axis=0)


def solution(mesh):
    placed = (
        P("seq", None),
        P("seq", "mp"),
        P("seq", "mp"),
        P("seq", "mp"),
        P(None, "mp", None),
        P(),
        P("mp", None),
        P(),
        P(None, "mp"),
        P("mp", None),
    )
    return jax.shard_map(
        local, mesh=mesh, in_specs=placed, out_specs=P("seq", "mp"), check_vma=False
    )
```

```python
import math

import jax
import jax.numpy as jnp
from jax import lax
from jax.sharding import PartitionSpec as P

HD = 64
BLK = 64
R = 3
GLOB = 2
GROUP = 16
QB_DEV = 16


def with_halo(block, sides, width):
    for axis, dim in sides:
        count = lax.axis_size(axis)
        forward = [(i, i + 1) for i in range(count - 1)]
        backward = [(target, source) for source, target in forward]
        low = lax.ppermute(
            lax.slice_in_dim(block, block.shape[dim] - width, None, axis=dim), axis, forward
        )
        high = lax.ppermute(lax.slice_in_dim(block, 0, width, axis=dim), axis, backward)
        block = jnp.concatenate([low, block, high], axis=dim)
    return block


def swapped(block, axis, apart):
    count = lax.axis_size(axis)
    route = []
    for low in range(count):
        high = low | 1 << apart
        if high != low and high < count:
            route += [(low, high), (high, low)]
    return lax.ppermute(block, axis, route)


def xor_partners(block, axis, low_bit, width):
    count = lax.axis_size(axis)
    return [
        lax.ppermute(block, axis, [(i, i ^ k << low_bit) for i in range(count)])
        for k in range(1, 1 << width)
    ]


def tree_stages(axis):
    bits = lax.axis_size(axis).bit_length() - 1
    return [(low, min(2, bits - low)) for low in range(0, bits, 2)]


def tree_sum(block, axis):
    stages = []
    for low_bit, width in reversed(tree_stages(axis)):
        for part in xor_partners(block, axis, low_bit, width):
            block = block + part
        stages.append(block)
    return block, stages


def merge_packed(parts):
    larger = parts[0][..., :1]
    for part in parts[1:]:
        larger = jnp.maximum(larger, part[..., :1])
    mixed = parts[0][..., 1:] * jnp.exp(parts[0][..., :1] - larger)
    for part in parts[1:]:
        mixed = mixed + part[..., 1:] * jnp.exp(part[..., :1] - larger)
    return jnp.concatenate([larger, mixed], axis=-1)


def tree_merge(packed, axis):
    for low_bit, width in tree_stages(axis):
        packed = merge_packed([packed] + xor_partners(packed, axis, low_bit, width))
    return packed


def local(
    residual_in,
    query_rows,
    key_rows,
    value_rows,
    rand_blocks,
    global_blocks,
    out_weight,
    norm_gain,
    up_weight,
    down_weight,
):
    tok_rows = query_rows.shape[0]
    local_width = query_rows.shape[1]
    heads_here = local_width // HD
    shard_count = lax.axis_size("seq")
    my_shard = lax.axis_index("seq")
    total_blocks = QB_DEV * shard_count
    score_scale = 1.0 / math.sqrt(HD)
    q_heads = query_rows.reshape(QB_DEV, BLK, heads_here, HD)
    key_heads = key_rows.reshape(tok_rows, heads_here, HD)
    value_heads = value_rows.reshape(tok_rows, heads_here, HD)
    kv_tokens = jnp.concatenate([key_heads, value_heads], axis=2)
    padded = with_halo(kv_tokens, (("seq", 0),), BLK)
    padded_blocks = padded.reshape(QB_DEV + 2, BLK, heads_here, 2 * HD).transpose(0, 2, 1, 3)
    own_blocks = padded_blocks[1:-1]
    window_kv = jnp.stack([padded_blocks[:-2], own_blocks, padded_blocks[2:]], axis=2)
    flat_kv = own_blocks.reshape(QB_DEV * heads_here, BLK, 2 * HD)
    position = my_shard % GROUP
    group_base = my_shard - position
    slot_count = QB_DEV * heads_here * R
    capacity = slot_count // GROUP
    offsets_all = jnp.arange(GROUP, dtype=jnp.int32)
    slot_heads = jnp.arange(slot_count, dtype=jnp.int32) // R % heads_here
    cap_range = jnp.arange(capacity, dtype=jnp.int32)

    def requests_of(shard):
        request_rows = lax.dynamic_slice_in_dim(rand_blocks, shard * QB_DEV, QB_DEV, 0)
        return request_rows.reshape(slot_count)

    def payload_for(offset):
        requester = group_base + (position - offset) % GROUP
        wanted = requests_of(requester)
        from_me = wanted // QB_DEV == my_shard
        order_rank = jnp.cumsum(from_me.astype(jnp.int32)) - 1
        source = wanted % QB_DEV * heads_here + slot_heads
        pick_table = from_me[:, None] & (order_rank[:, None] == cap_range[None, :])
        chosen = jnp.sum(jnp.where(pick_table, source[:, None], 0), axis=0)
        return jnp.take(flat_kv, chosen, axis=0)

    my_requests = requests_of(my_shard)
    owner_offset = (my_requests // QB_DEV - group_base - position) % GROUP
    offset_hits = owner_offset[:, None] == offsets_all[None, :]
    rank_table = jnp.cumsum(offset_hits.astype(jnp.int32), axis=0) - 1
    my_rank = jnp.sum(jnp.where(offset_hits, rank_table, 0), axis=1)
    slot_index = owner_offset * capacity + my_rank
    sectioned = jax.vmap(payload_for)(offsets_all)
    packed = jnp.stack([query_rows, key_rows, value_rows], axis=0)
    contributions = []
    for which in range(GLOB):
        global_id = global_blocks[which]
        block_rows = lax.dynamic_slice_in_dim(packed, global_id % QB_DEV * BLK, BLK, 1)
        is_owner = global_id // QB_DEV == my_shard
        contributions.append(jnp.where(is_owner, block_rows, jnp.zeros_like(block_rows)))
    global_packed, tree_steps = tree_sum(jnp.stack(contributions, axis=0), "seq")
    mp_index = lax.axis_index("mp")
    mp_route = [(0, 1), (1, 0)]
    half_width = residual_in.shape[1] // lax.axis_size("mp")
    other_index = 1 - mp_index
    their_down = lax.dynamic_slice_in_dim(down_weight, other_index * half_width, half_width, 1)
    _, late_up, late_down, late_out = lax.optimization_barrier(
        (tree_steps[0], up_weight, their_down, out_weight)
    )
    other_up = lax.ppermute(late_up, "mp", mp_route)
    other_down = lax.ppermute(late_down, "mp", mp_route)
    other_weight = lax.ppermute(late_out, "mp", mp_route)
    sectioned, _ = lax.optimization_barrier((sectioned, tree_steps[1]))
    shard_ids = range(shard_count)
    arrived = [sectioned[0]]
    for offset in range(1, GROUP):
        route = [(s, s - s % GROUP + (s % GROUP - offset) % GROUP) for s in shard_ids]
        arrived.append(lax.ppermute(sectioned[offset], "seq", route))
    received = jnp.stack(arrived, axis=0)
    random_kv = jnp.take(received.reshape(GROUP * capacity, BLK, 2 * HD), slot_index, axis=0)
    random_kv = random_kv.reshape(QB_DEV, heads_here, R, BLK, 2 * HD)
    global_q = global_packed[:, 0].reshape(GLOB, BLK, heads_here, HD)
    global_k = global_packed[:, 1].reshape(GLOB, BLK, heads_here, HD)
    global_v = global_packed[:, 2].reshape(GLOB, BLK, heads_here, HD)
    global_kv = jnp.concatenate([global_k, global_v], axis=3).transpose(2, 0, 1, 3)
    global_kv = jnp.broadcast_to(global_kv[None], (QB_DEV, heads_here, GLOB, BLK, 2 * HD))
    all_kv = jnp.concatenate([window_kv, random_kv, global_kv], axis=2)
    keys_all = all_kv[..., :HD]
    values_all = all_kv[..., HD:]
    scores = (
        jnp.einsum("bqhd,bhjkd->bhqjk", q_heads, keys_all, preferred_element_type=jnp.float32)
        * score_scale
    )
    block_global = my_shard * QB_DEV + jnp.arange(QB_DEV, dtype=jnp.int32)
    valid_cols = jnp.concatenate(
        [
            (block_global >= 1)[:, None],
            jnp.ones((QB_DEV, 1), dtype=bool),
            (block_global + 1 < total_blocks)[:, None],
            jnp.ones((QB_DEV, R + GLOB), dtype=bool),
        ],
        axis=1,
    )
    scores = jnp.where(valid_cols[:, None, None, :, None], scores, jnp.float32(-1e30))
    row_peak = jnp.max(scores, axis=(3, 4), keepdims=True)
    weights = jnp.exp(scores - row_peak)
    row_total = jnp.sum(weights, axis=(3, 4))
    mixed_sum = jnp.einsum(
        "bhqjk,bhjkd->bqhd",
        weights.astype(jnp.bfloat16),
        values_all,
        preferred_element_type=jnp.float32,
    )
    sparse_out = mixed_sum / row_total.transpose(0, 2, 1)[..., None]
    global_scores = (
        jnp.einsum("gqhd,thd->ghqt", global_q, key_heads, preferred_element_type=jnp.float32)
        * score_scale
    )
    seg_peak = jnp.max(global_scores, axis=3)
    seg_weights = jnp.exp(global_scores - seg_peak[..., None])
    seg_total = jnp.sum(seg_weights, axis=3)
    seg_acc = jnp.einsum(
        "ghqt,thd->ghqd",
        seg_weights.astype(jnp.bfloat16),
        value_heads,
        preferred_element_type=jnp.float32,
    )
    seg_packed = jnp.concatenate([seg_peak[..., None], seg_total[..., None], seg_acc], axis=-1)
    merged = tree_merge(seg_packed, "seq")
    global_out = merged[..., 2:] / merged[..., 1:2]
    attn_rows = sparse_out.reshape(tok_rows, local_width)
    for which in range(GLOB):
        global_id = global_blocks[which]
        start_row = global_id % QB_DEV * BLK
        current = lax.dynamic_slice_in_dim(attn_rows, start_row, BLK, 0)
        replacing = global_out[which].transpose(1, 0, 2).reshape(BLK, local_width)
        is_owner = global_id // QB_DEV == my_shard
        attn_rows = lax.dynamic_update_slice_in_dim(
            attn_rows, jnp.where(is_owner, replacing, current), start_row, 0
        )
    attention = attn_rows.astype(jnp.bfloat16)
    attention, other_up, other_down = lax.optimization_barrier((attention, other_up, other_down))
    other_attention = lax.ppermute(attention, "mp", mp_route)
    projected = jnp.dot(attention, out_weight, preferred_element_type=jnp.float32) + jnp.dot(
        other_attention, other_weight, preferred_element_type=jnp.float32
    )
    middle = (residual_in.astype(jnp.float32) + projected).astype(jnp.bfloat16)
    middle_own = lax.dynamic_slice_in_dim(middle, mp_index * half_width, half_width, 1)
    middle32 = middle.astype(jnp.float32)
    row_mean = jnp.mean(middle32, axis=1, keepdims=True)
    centered = middle32 - row_mean
    row_var = jnp.mean(centered * centered, axis=1, keepdims=True)
    normed = (centered * lax.rsqrt(row_var + 1e-05) * norm_gain).astype(jnp.bfloat16)
    own_down = lax.dynamic_slice_in_dim(down_weight, mp_index * half_width, half_width, 1)
    hidden_own = jax.nn.gelu(
        jnp.dot(normed, up_weight, preferred_element_type=jnp.float32), approximate=True
    ).astype(jnp.bfloat16)
    hidden_other = jax.nn.gelu(
        jnp.dot(normed, other_up, preferred_element_type=jnp.float32), approximate=True
    ).astype(jnp.bfloat16)
    down_part = jnp.dot(hidden_own, own_down, preferred_element_type=jnp.float32) + jnp.dot(
        hidden_other, other_down, preferred_element_type=jnp.float32
    )
    return (middle_own.astype(jnp.float32) + down_part).astype(jnp.bfloat16)


def solution(mesh):
    placed = (
        P("seq", None),
        P("seq", "mp"),
        P("seq", "mp"),
        P("seq", "mp"),
        P(None, "mp", None),
        P(),
        P("mp", None),
        P(),
        P(None, "mp"),
        P("mp", None),
    )
    return jax.shard_map(
        local, mesh=mesh, in_specs=placed, out_specs=P("seq", "mp"), check_vma=False
    )
```

```python
import math

import jax
import jax.numpy as jnp
from jax import lax
from jax.sharding import PartitionSpec as P

HD = 64
BLK = 64
R = 3
GLOB = 2
GROUP = 16
QB_DEV = 16


def with_halo(block, sides, width):
    for axis, dim in sides:
        count = lax.axis_size(axis)
        forward = [(i, i + 1) for i in range(count - 1)]
        backward = [(target, source) for source, target in forward]
        low = lax.ppermute(
            lax.slice_in_dim(block, block.shape[dim] - width, None, axis=dim), axis, forward
        )
        high = lax.ppermute(lax.slice_in_dim(block, 0, width, axis=dim), axis, backward)
        block = jnp.concatenate([low, block, high], axis=dim)
    return block


def swapped(block, axis, apart):
    count = lax.axis_size(axis)
    route = []
    for low in range(count):
        high = low | 1 << apart
        if high != low and high < count:
            route += [(low, high), (high, low)]
    return lax.ppermute(block, axis, route)


def xor_partners(block, axis, low_bit, width):
    count = lax.axis_size(axis)
    return [
        lax.ppermute(block, axis, [(i, i ^ k << low_bit) for i in range(count)])
        for k in range(1, 1 << width)
    ]


def tree_stages(axis):
    bits = lax.axis_size(axis).bit_length() - 1
    return [(low, min(2, bits - low)) for low in range(0, bits, 2)]


def tree_sum(block, axis):
    stages = []
    for low_bit, width in reversed(tree_stages(axis)):
        for part in xor_partners(block, axis, low_bit, width):
            block = block + part
        stages.append(block)
    return block, stages


def merge_packed(parts):
    larger = parts[0][..., :1]
    for part in parts[1:]:
        larger = jnp.maximum(larger, part[..., :1])
    mixed = parts[0][..., 1:] * jnp.exp(parts[0][..., :1] - larger)
    for part in parts[1:]:
        mixed = mixed + part[..., 1:] * jnp.exp(part[..., :1] - larger)
    return jnp.concatenate([larger, mixed], axis=-1)


def tree_merge(packed, axis):
    for low_bit, width in tree_stages(axis):
        packed = merge_packed([packed] + xor_partners(packed, axis, low_bit, width))
    return packed


def local(
    residual_in,
    query_rows,
    key_rows,
    value_rows,
    rand_blocks,
    global_blocks,
    out_weight,
    norm_gain,
    up_weight,
    down_weight,
):
    tok_rows = query_rows.shape[0]
    local_width = query_rows.shape[1]
    heads_here = local_width // HD
    shard_count = lax.axis_size("seq")
    my_shard = lax.axis_index("seq")
    total_blocks = QB_DEV * shard_count
    score_scale = 1.0 / math.sqrt(HD)
    q_heads = query_rows.reshape(QB_DEV, BLK, heads_here, HD)
    key_heads = key_rows.reshape(tok_rows, heads_here, HD)
    value_heads = value_rows.reshape(tok_rows, heads_here, HD)
    kv_tokens = jnp.concatenate([key_heads, value_heads], axis=2)
    padded = with_halo(kv_tokens, (("seq", 0),), BLK)
    padded_blocks = padded.reshape(QB_DEV + 2, BLK, heads_here, 2 * HD).transpose(0, 2, 1, 3)
    own_blocks = padded_blocks[1:-1]
    window_kv = jnp.stack([padded_blocks[:-2], own_blocks, padded_blocks[2:]], axis=2)
    flat_kv = own_blocks.reshape(QB_DEV * heads_here, BLK, 2 * HD)
    position = my_shard % GROUP
    group_base = my_shard - position
    slot_count = QB_DEV * heads_here * R
    capacity = slot_count // GROUP
    offsets_all = jnp.arange(GROUP, dtype=jnp.int32)
    slot_heads = jnp.arange(slot_count, dtype=jnp.int32) // R % heads_here
    cap_range = jnp.arange(capacity, dtype=jnp.int32)

    def requests_of(shard):
        request_rows = lax.dynamic_slice_in_dim(rand_blocks, shard * QB_DEV, QB_DEV, 0)
        return request_rows.reshape(slot_count)

    def payload_for(offset):
        requester = group_base + (position - offset) % GROUP
        wanted = requests_of(requester)
        from_me = wanted // QB_DEV == my_shard
        order_rank = jnp.cumsum(from_me.astype(jnp.int32)) - 1
        source = wanted % QB_DEV * heads_here + slot_heads
        pick_table = from_me[:, None] & (order_rank[:, None] == cap_range[None, :])
        chosen = jnp.sum(jnp.where(pick_table, source[:, None], 0), axis=0)
        return jnp.take(flat_kv, chosen, axis=0)

    my_requests = requests_of(my_shard)
    owner_offset = (my_requests // QB_DEV - group_base - position) % GROUP
    offset_hits = owner_offset[:, None] == offsets_all[None, :]
    rank_table = jnp.cumsum(offset_hits.astype(jnp.int32), axis=0) - 1
    my_rank = jnp.sum(jnp.where(offset_hits, rank_table, 0), axis=1)
    slot_index = owner_offset * capacity + my_rank
    sectioned = jax.vmap(payload_for)(offsets_all)
    packed = jnp.stack([query_rows, key_rows, value_rows], axis=0)
    contributions = []
    for which in range(GLOB):
        global_id = global_blocks[which]
        block_rows = lax.dynamic_slice_in_dim(packed, global_id % QB_DEV * BLK, BLK, 1)
        is_owner = global_id // QB_DEV == my_shard
        contributions.append(jnp.where(is_owner, block_rows, jnp.zeros_like(block_rows)))
    global_packed, tree_steps = tree_sum(jnp.stack(contributions, axis=0), "seq")
    mp_index = lax.axis_index("mp")
    mp_route = [(0, 1), (1, 0)]
    half_width = residual_in.shape[1] // lax.axis_size("mp")
    other_index = 1 - mp_index
    their_down = lax.dynamic_slice_in_dim(down_weight, other_index * half_width, half_width, 1)
    _, late_up, late_down, late_out = lax.optimization_barrier(
        (tree_steps[0], up_weight, their_down, out_weight)
    )
    other_up = lax.ppermute(late_up, "mp", mp_route)
    other_down = lax.ppermute(late_down, "mp", mp_route)
    other_weight = lax.ppermute(late_out, "mp", mp_route)
    sectioned, _ = lax.optimization_barrier((sectioned, tree_steps[1]))
    shard_ids = range(shard_count)
    arrived = [sectioned[0]]
    for offset in range(1, GROUP):
        route = [(s, s - s % GROUP + (s % GROUP - offset) % GROUP) for s in shard_ids]
        arrived.append(lax.ppermute(sectioned[offset], "seq", route))
    received = jnp.stack(arrived, axis=0)
    random_kv = jnp.take(received.reshape(GROUP * capacity, BLK, 2 * HD), slot_index, axis=0)
    random_kv = random_kv.reshape(QB_DEV, heads_here, R, BLK, 2 * HD)
    global_q = global_packed[:, 0].reshape(GLOB, BLK, heads_here, HD)
    global_k = global_packed[:, 1].reshape(GLOB, BLK, heads_here, HD)
    global_v = global_packed[:, 2].reshape(GLOB, BLK, heads_here, HD)
    global_kv = jnp.concatenate([global_k, global_v], axis=3).transpose(2, 0, 1, 3)
    global_kv = jnp.broadcast_to(global_kv[None], (QB_DEV, heads_here, GLOB, BLK, 2 * HD))
    all_kv = jnp.concatenate([window_kv, random_kv, global_kv], axis=2)
    keys_all = all_kv[..., :HD]
    values_all = all_kv[..., HD:]
    scores = (
        jnp.einsum("bqhd,bhjkd->bhqjk", q_heads, keys_all, preferred_element_type=jnp.float32)
        * score_scale
    )
    block_global = my_shard * QB_DEV + jnp.arange(QB_DEV, dtype=jnp.int32)
    valid_cols = jnp.concatenate(
        [
            (block_global >= 1)[:, None],
            jnp.ones((QB_DEV, 1), dtype=bool),
            (block_global + 1 < total_blocks)[:, None],
            jnp.ones((QB_DEV, R + GLOB), dtype=bool),
        ],
        axis=1,
    )
    scores = jnp.where(valid_cols[:, None, None, :, None], scores, jnp.float32(-1e30))
    row_peak = jnp.max(scores, axis=(3, 4), keepdims=True)
    weights = jnp.exp(scores - row_peak)
    row_total = jnp.sum(weights, axis=(3, 4))
    mixed_sum = jnp.einsum(
        "bhqjk,bhjkd->bqhd",
        weights.astype(jnp.bfloat16),
        values_all,
        preferred_element_type=jnp.float32,
    )
    sparse_out = mixed_sum / row_total.transpose(0, 2, 1)[..., None]
    global_scores = (
        jnp.einsum("gqhd,thd->ghqt", global_q, key_heads, preferred_element_type=jnp.float32)
        * score_scale
    )
    seg_peak = jnp.max(global_scores, axis=3)
    seg_weights = jnp.exp(global_scores - seg_peak[..., None])
    seg_total = jnp.sum(seg_weights, axis=3)
    seg_acc = jnp.einsum(
        "ghqt,thd->ghqd",
        seg_weights.astype(jnp.bfloat16),
        value_heads,
        preferred_element_type=jnp.float32,
    )
    seg_packed = jnp.concatenate([seg_peak[..., None], seg_total[..., None], seg_acc], axis=-1)
    merged = tree_merge(seg_packed, "seq")
    global_out = merged[..., 2:] / merged[..., 1:2]
    attn_rows = sparse_out.reshape(tok_rows, local_width)
    for which in range(GLOB):
        global_id = global_blocks[which]
        start_row = global_id % QB_DEV * BLK
        current = lax.dynamic_slice_in_dim(attn_rows, start_row, BLK, 0)
        replacing = global_out[which].transpose(1, 0, 2).reshape(BLK, local_width)
        is_owner = global_id // QB_DEV == my_shard
        attn_rows = lax.dynamic_update_slice_in_dim(
            attn_rows, jnp.where(is_owner, replacing, current), start_row, 0
        )
    attention = attn_rows.astype(jnp.bfloat16)
    attention, other_up, other_down = lax.optimization_barrier((attention, other_up, other_down))
    own_down = lax.dynamic_slice_in_dim(down_weight, mp_index * half_width, half_width, 1)
    chunk_rows = tok_rows // 2
    results = []
    for first_row in range(0, tok_rows, chunk_rows):
        mine = lax.slice_in_dim(attention, first_row, first_row + chunk_rows, axis=0)
        theirs = lax.ppermute(mine, "mp", mp_route)
        projected = jnp.dot(mine, out_weight, preferred_element_type=jnp.float32) + jnp.dot(
            theirs, other_weight, preferred_element_type=jnp.float32
        )
        residual = lax.slice_in_dim(residual_in, first_row, first_row + chunk_rows, axis=0)
        middle = (residual.astype(jnp.float32) + projected).astype(jnp.bfloat16)
        middle_own = lax.dynamic_slice_in_dim(middle, mp_index * half_width, half_width, 1)
        middle32 = middle.astype(jnp.float32)
        row_mean = jnp.mean(middle32, axis=1, keepdims=True)
        centered = middle32 - row_mean
        row_var = jnp.mean(centered * centered, axis=1, keepdims=True)
        normed = (centered * lax.rsqrt(row_var + 1e-05) * norm_gain).astype(jnp.bfloat16)
        hidden_own = jax.nn.gelu(
            jnp.dot(normed, up_weight, preferred_element_type=jnp.float32), approximate=True
        ).astype(jnp.bfloat16)
        hidden_other = jax.nn.gelu(
            jnp.dot(normed, other_up, preferred_element_type=jnp.float32), approximate=True
        ).astype(jnp.bfloat16)
        down_part = jnp.dot(hidden_own, own_down, preferred_element_type=jnp.float32) + jnp.dot(
            hidden_other, other_down, preferred_element_type=jnp.float32
        )
        results.append((middle_own.astype(jnp.float32) + down_part).astype(jnp.bfloat16))
    return jnp.concatenate(results, axis=0)


def solution(mesh):
    placed = (
        P("seq", None),
        P("seq", "mp"),
        P("seq", "mp"),
        P("seq", "mp"),
        P(None, "mp", None),
        P(),
        P("mp", None),
        P(),
        P(None, "mp"),
        P("mp", None),
    )
    return jax.shard_map(
        local, mesh=mesh, in_specs=placed, out_specs=P("seq", "mp"), check_vma=False
    )
```

```python
import math

import jax
import jax.numpy as jnp
from jax import lax
from jax.sharding import PartitionSpec as P

HD = 64
BLK = 64
R = 3
GLOB = 2
GROUP = 16
QB_DEV = 16


def with_halo(block, sides, width):
    for axis, dim in sides:
        count = lax.axis_size(axis)
        forward = [(i, i + 1) for i in range(count - 1)]
        backward = [(target, source) for source, target in forward]
        low = lax.ppermute(
            lax.slice_in_dim(block, block.shape[dim] - width, None, axis=dim), axis, forward
        )
        high = lax.ppermute(lax.slice_in_dim(block, 0, width, axis=dim), axis, backward)
        block = jnp.concatenate([low, block, high], axis=dim)
    return block


def swapped(block, axis, apart):
    count = lax.axis_size(axis)
    route = []
    for low in range(count):
        high = low | 1 << apart
        if high != low and high < count:
            route += [(low, high), (high, low)]
    return lax.ppermute(block, axis, route)


def xor_partners(block, axis, low_bit, width):
    count = lax.axis_size(axis)
    return [
        lax.ppermute(block, axis, [(i, i ^ k << low_bit) for i in range(count)])
        for k in range(1, 1 << width)
    ]


def tree_stages(axis):
    bits = lax.axis_size(axis).bit_length() - 1
    return [(low, min(2, bits - low)) for low in range(0, bits, 2)]


def tree_sum(block, axis):
    stages = []
    for low_bit, width in reversed(tree_stages(axis)):
        for part in xor_partners(block, axis, low_bit, width):
            block = block + part
        stages.append(block)
    return block, stages


def merge_packed(parts):
    larger = parts[0][..., :1]
    for part in parts[1:]:
        larger = jnp.maximum(larger, part[..., :1])
    mixed = parts[0][..., 1:] * jnp.exp(parts[0][..., :1] - larger)
    for part in parts[1:]:
        mixed = mixed + part[..., 1:] * jnp.exp(part[..., :1] - larger)
    return jnp.concatenate([larger, mixed], axis=-1)


def tree_merge(packed, axis):
    for low_bit in range(lax.axis_size(axis).bit_length() - 1):
        width = 1
        packed = merge_packed([packed] + xor_partners(packed, axis, low_bit, width))
    return packed


def local(
    residual_in,
    query_rows,
    key_rows,
    value_rows,
    rand_blocks,
    global_blocks,
    out_weight,
    norm_gain,
    up_weight,
    down_weight,
):
    tok_rows = query_rows.shape[0]
    local_width = query_rows.shape[1]
    heads_here = local_width // HD
    shard_count = lax.axis_size("seq")
    my_shard = lax.axis_index("seq")
    total_blocks = QB_DEV * shard_count
    score_scale = 1.0 / math.sqrt(HD)
    q_heads = query_rows.reshape(QB_DEV, BLK, heads_here, HD)
    key_heads = key_rows.reshape(tok_rows, heads_here, HD)
    value_heads = value_rows.reshape(tok_rows, heads_here, HD)
    kv_tokens = jnp.concatenate([key_heads, value_heads], axis=2)
    padded = with_halo(kv_tokens, (("seq", 0),), BLK)
    padded_blocks = padded.reshape(QB_DEV + 2, BLK, heads_here, 2 * HD).transpose(0, 2, 1, 3)
    own_blocks = padded_blocks[1:-1]
    window_kv = jnp.stack([padded_blocks[:-2], own_blocks, padded_blocks[2:]], axis=2)
    flat_kv = own_blocks.reshape(QB_DEV * heads_here, BLK, 2 * HD)
    position = my_shard % GROUP
    group_base = my_shard - position
    slot_count = QB_DEV * heads_here * R
    capacity = slot_count // GROUP
    offsets_all = jnp.arange(GROUP, dtype=jnp.int32)
    slot_heads = jnp.arange(slot_count, dtype=jnp.int32) // R % heads_here
    cap_range = jnp.arange(capacity, dtype=jnp.int32)

    def requests_of(shard):
        request_rows = lax.dynamic_slice_in_dim(rand_blocks, shard * QB_DEV, QB_DEV, 0)
        return request_rows.reshape(slot_count)

    def payload_for(offset):
        requester = group_base + (position - offset) % GROUP
        wanted = requests_of(requester)
        from_me = wanted // QB_DEV == my_shard
        order_rank = jnp.cumsum(from_me.astype(jnp.int32)) - 1
        source = wanted % QB_DEV * heads_here + slot_heads
        pick_table = from_me[:, None] & (order_rank[:, None] == cap_range[None, :])
        chosen = jnp.sum(jnp.where(pick_table, source[:, None], 0), axis=0)
        return jnp.take(flat_kv, chosen, axis=0)

    my_requests = requests_of(my_shard)
    owner_offset = (my_requests // QB_DEV - group_base - position) % GROUP
    offset_hits = owner_offset[:, None] == offsets_all[None, :]
    rank_table = jnp.cumsum(offset_hits.astype(jnp.int32), axis=0) - 1
    my_rank = jnp.sum(jnp.where(offset_hits, rank_table, 0), axis=1)
    slot_index = owner_offset * capacity + my_rank
    sectioned = jax.vmap(payload_for)(offsets_all)
    packed = jnp.stack([query_rows, key_rows, value_rows], axis=0)
    contributions = []
    for which in range(GLOB):
        global_id = global_blocks[which]
        block_rows = lax.dynamic_slice_in_dim(packed, global_id % QB_DEV * BLK, BLK, 1)
        is_owner = global_id // QB_DEV == my_shard
        contributions.append(jnp.where(is_owner, block_rows, jnp.zeros_like(block_rows)))
    global_packed, tree_steps = tree_sum(jnp.stack(contributions, axis=0), "seq")
    mp_index = lax.axis_index("mp")
    mp_route = [(0, 1), (1, 0)]
    half_width = residual_in.shape[1] // lax.axis_size("mp")
    other_index = 1 - mp_index
    their_down = lax.dynamic_slice_in_dim(down_weight, other_index * half_width, half_width, 1)
    _, late_up, late_down, late_out = lax.optimization_barrier(
        (tree_steps[0], up_weight, their_down, out_weight)
    )
    other_up = lax.ppermute(late_up, "mp", mp_route)
    other_down = lax.ppermute(late_down, "mp", mp_route)
    other_weight = lax.ppermute(late_out, "mp", mp_route)
    sectioned, _ = lax.optimization_barrier((sectioned, tree_steps[1]))
    shard_ids = range(shard_count)
    arrived = [sectioned[0]]
    for offset in range(1, GROUP):
        route = [(s, s - s % GROUP + (s % GROUP - offset) % GROUP) for s in shard_ids]
        arrived.append(lax.ppermute(sectioned[offset], "seq", route))
    received = jnp.stack(arrived, axis=0)
    random_kv = jnp.take(received.reshape(GROUP * capacity, BLK, 2 * HD), slot_index, axis=0)
    random_kv = random_kv.reshape(QB_DEV, heads_here, R, BLK, 2 * HD)
    global_q = global_packed[:, 0].reshape(GLOB, BLK, heads_here, HD)
    global_k = global_packed[:, 1].reshape(GLOB, BLK, heads_here, HD)
    global_v = global_packed[:, 2].reshape(GLOB, BLK, heads_here, HD)
    global_kv = jnp.concatenate([global_k, global_v], axis=3).transpose(2, 0, 1, 3)
    global_kv = jnp.broadcast_to(global_kv[None], (QB_DEV, heads_here, GLOB, BLK, 2 * HD))
    all_kv = jnp.concatenate([window_kv, random_kv, global_kv], axis=2)
    keys_all = all_kv[..., :HD]
    values_all = all_kv[..., HD:]
    scores = (
        jnp.einsum("bqhd,bhjkd->bhqjk", q_heads, keys_all, preferred_element_type=jnp.float32)
        * score_scale
    )
    block_global = my_shard * QB_DEV + jnp.arange(QB_DEV, dtype=jnp.int32)
    valid_cols = jnp.concatenate(
        [
            (block_global >= 1)[:, None],
            jnp.ones((QB_DEV, 1), dtype=bool),
            (block_global + 1 < total_blocks)[:, None],
            jnp.ones((QB_DEV, R + GLOB), dtype=bool),
        ],
        axis=1,
    )
    scores = jnp.where(valid_cols[:, None, None, :, None], scores, jnp.float32(-1e30))
    row_peak = jnp.max(scores, axis=(3, 4), keepdims=True)
    weights = jnp.exp(scores - row_peak)
    row_total = jnp.sum(weights, axis=(3, 4))
    mixed_sum = jnp.einsum(
        "bhqjk,bhjkd->bqhd",
        weights.astype(jnp.bfloat16),
        values_all,
        preferred_element_type=jnp.float32,
    )
    sparse_out = mixed_sum / row_total.transpose(0, 2, 1)[..., None]
    global_scores = (
        jnp.einsum("gqhd,thd->ghqt", global_q, key_heads, preferred_element_type=jnp.float32)
        * score_scale
    )
    seg_peak = jnp.max(global_scores, axis=3)
    seg_weights = jnp.exp(global_scores - seg_peak[..., None])
    seg_total = jnp.sum(seg_weights, axis=3)
    seg_acc = jnp.einsum(
        "ghqt,thd->ghqd",
        seg_weights.astype(jnp.bfloat16),
        value_heads,
        preferred_element_type=jnp.float32,
    )
    seg_packed = jnp.concatenate([seg_peak[..., None], seg_total[..., None], seg_acc], axis=-1)
    merged = tree_merge(seg_packed, "seq")
    global_out = merged[..., 2:] / merged[..., 1:2]
    attn_rows = sparse_out.reshape(tok_rows, local_width)
    for which in range(GLOB):
        global_id = global_blocks[which]
        start_row = global_id % QB_DEV * BLK
        current = lax.dynamic_slice_in_dim(attn_rows, start_row, BLK, 0)
        replacing = global_out[which].transpose(1, 0, 2).reshape(BLK, local_width)
        is_owner = global_id // QB_DEV == my_shard
        attn_rows = lax.dynamic_update_slice_in_dim(
            attn_rows, jnp.where(is_owner, replacing, current), start_row, 0
        )
    attention = attn_rows.astype(jnp.bfloat16)
    attention, other_up, other_down = lax.optimization_barrier((attention, other_up, other_down))
    other_attention = lax.ppermute(attention, "mp", mp_route)
    projected = jnp.dot(attention, out_weight, preferred_element_type=jnp.float32) + jnp.dot(
        other_attention, other_weight, preferred_element_type=jnp.float32
    )
    middle = (residual_in.astype(jnp.float32) + projected).astype(jnp.bfloat16)
    middle_own = lax.dynamic_slice_in_dim(middle, mp_index * half_width, half_width, 1)
    middle32 = middle.astype(jnp.float32)
    row_mean = jnp.mean(middle32, axis=1, keepdims=True)
    centered = middle32 - row_mean
    row_var = jnp.mean(centered * centered, axis=1, keepdims=True)
    normed = (centered * lax.rsqrt(row_var + 1e-05) * norm_gain).astype(jnp.bfloat16)
    own_down = lax.dynamic_slice_in_dim(down_weight, mp_index * half_width, half_width, 1)
    hidden_own = jax.nn.gelu(
        jnp.dot(normed, up_weight, preferred_element_type=jnp.float32), approximate=True
    ).astype(jnp.bfloat16)
    hidden_other = jax.nn.gelu(
        jnp.dot(normed, other_up, preferred_element_type=jnp.float32), approximate=True
    ).astype(jnp.bfloat16)
    down_part = jnp.dot(hidden_own, own_down, preferred_element_type=jnp.float32) + jnp.dot(
        hidden_other, other_down, preferred_element_type=jnp.float32
    )
    return (middle_own.astype(jnp.float32) + down_part).astype(jnp.bfloat16)


def solution(mesh):
    placed = (
        P("seq", None),
        P("seq", "mp"),
        P("seq", "mp"),
        P("seq", "mp"),
        P(None, "mp", None),
        P(),
        P("mp", None),
        P(),
        P(None, "mp"),
        P("mp", None),
    )
    return jax.shard_map(
        local, mesh=mesh, in_specs=placed, out_specs=P("seq", "mp"), check_vma=False
    )
```
